256 devices in a mesh: dp: 4 (over x), ctx: 16 (over z, y_hi), tp: 4 (over y_lo, core).
Axes of the slice: x: 4, y: 4 (y_hi: 2, y_lo: 2; y = y_hi * 2 + y_lo), z: 8, core: 2. Of those that a mesh axis runs over, the one named last changes fastest.
Arguments:
- query_rows: bfloat16 [16384, 4096], P(('dp', 'ctx'), 'tp'), parts along dimension 0, may hold values from -6 to 6
- key_matrix: bfloat16 [16384, 512], P(('dp', 'ctx'), 'tp'), parts along dimension 0, may hold values from -6 to 6
- value_matrix: bfloat16 [16384, 512], P(('dp', 'ctx'), 'tp'), parts along dimension 0, may hold values from -6 to 6
- attn_out: bfloat16 [16384, 4096], P(('dp', 'ctx'), 'tp'), parts along dimension 0, may hold values from -6 to 6
- out_grad: bfloat16 [16384, 4096], P(('dp', 'ctx', 'tp')), parts along dimension 0, may hold values from -0.5 to 0.5
- log_sums: float32 [32, 16384], P('tp', ('dp', 'ctx')), parts along dimension 1, may hold values from 3 to 5
- block_mask: int32 [128, 32], P('dp'), parts along dimension 0, may hold values 0 or 1
Outputs:
- query_grad: bfloat16 [16384, 4096], P(('dp', 'ctx'), 'tp'), parts along dimension 0
- key_gradient: bfloat16 [16384, 512], P(('dp', 'ctx'), 'tp'), parts along dimension 0
- value_gradient: bfloat16 [16384, 512], P(('dp', 'ctx'), 'tp'), parts along dimension 0
The draws below stay inside these ranges and needn't reach their ends.
There are 4 independent parts, one for each index of `dp`. The reference program is written for one: setup_inputs(seed, part) draws one part's arguments, and reference() takes and returns one part's arrays. A program takes and returns all parts, laid end to end along the dimension named above; each array names one. Nothing has to cross between parts.
Inputs may be any that keep to these rules, and one draw needn't show every extreme that they name: `block_mask`: entry [a, b] with b < a lets query block a see key block b; entries on and above the diagonal are never read.
All inputs are finite; a program needn't handle non-finite values.
Results may differ from the reference program's by a relative error of at most 0.0049.
Values may be sent and summed in bfloat16 or wider, within the bound.
No kernel may reach another device: no remote copies, remote signals or barrier semaphores. Data moves between devices by JAX's collectives and lax.ppermute only.
A program may use at most 64 MiB of HBM per device.

```python
import math
import jax
import jax.numpy as jnp
from jax import lax

BLK = 128
HEAD_SIZE = 128
QUERY_PER_KEY = 8
KEY_VALUE_HEADS = 4
HQ = 32
TOKEN_COUNT = 4096
NB = 32


def place_ends(result, own_key, smallest, high):
    spot = [jax.random.randint(jax.random.fold_in(own_key, axis), (), 0, length) for axis, length in enumerate(result.shape)]
    widest = result.shape.index(max(result.shape))
    neighbour = spot[:widest] + [(spot[widest] + 1) % result.shape[widest]] + spot[widest + 1:]
    return result.at[tuple(spot)].set(smallest).at[tuple(neighbour)].set(high)


def levels(stream_key, dims, cuts, least, largest):
    factor_of = 1.0
    for position, parts in cuts:
        steps = jax.random.uniform(jax.random.fold_in(jax.random.fold_in(stream_key, 6), position), (parts,), jnp.float32, least / len(cuts), largest / len(cuts))
        factor_of = factor_of * jnp.repeat(jnp.exp(steps), dims[position] // parts).reshape((-1,) + (1,) * (len(dims) - 1 - position))
    return factor_of


def bell_draw(own_key, shape, spread, most, cuts=(), held_as=jnp.bfloat16):
    drawn = jax.random.normal(own_key, shape, jnp.float32) * spread
    if len(cuts) > 0:
        drawn = levels(own_key, shape, cuts, -0.22, 0.18) * drawn
    return jnp.clip(drawn, min=-most, max=most).astype(held_as)


def setup_inputs(seed: int = 0, part: int = 0) -> dict:
    seeds = jax.random.split(jax.random.key(seed), 8)
    part_splits = jax.random.split(jax.random.fold_in(seeds[7], part), 8)
    query_rows = bell_draw(part_splits[0], (TOKEN_COUNT, HQ * HEAD_SIZE), 1.0, 6.0, ((0, 16), (1, 4)))
    key_matrix = bell_draw(part_splits[1], (TOKEN_COUNT, KEY_VALUE_HEADS * HEAD_SIZE), 1.0, 6.0, ((0, 16), (1, 4)))
    value_matrix = bell_draw(part_splits[2], (TOKEN_COUNT, KEY_VALUE_HEADS * HEAD_SIZE), 1.0, 6.0, ((0, 16), (1, 4)))
    attn_out = bell_draw(part_splits[3], (TOKEN_COUNT, HQ * HEAD_SIZE), 1.0, 6.0, ((0, 16), (1, 4)))
    out_grad = bell_draw(part_splits[4], (TOKEN_COUNT, HQ * HEAD_SIZE), HEAD_SIZE ** -0.5, 0.5, ((0, 64),))
    log_sums = jnp.clip(3.0 + 2.0 * jax.random.uniform(part_splits[5], (HQ, TOKEN_COUNT), jnp.float32) ** levels(part_splits[5], (HQ, TOKEN_COUNT), ((0, 4), (1, 16)), -0.2, 0.2), 3.0, 5.0)
    block_mask = place_ends((jax.random.randint(part_splits[6], (NB, NB), 0, 4) < 3).astype(jnp.int32), jax.random.fold_in(part_splits[6], 1), 0, 1)
    return dict(query_rows=query_rows, key_matrix=key_matrix, value_matrix=value_matrix, attn_out=attn_out, out_grad=out_grad, log_sums=log_sums, block_mask=block_mask)


def reference(query_rows, key_matrix, value_matrix, attn_out, out_grad, log_sums, block_mask):
    logit_scale = 1.0 / math.sqrt(HEAD_SIZE)
    queries = query_rows.reshape(TOKEN_COUNT, HQ, HEAD_SIZE).astype(jnp.float32)
    grad_heads = out_grad.reshape(TOKEN_COUNT, HQ, HEAD_SIZE).astype(jnp.float32)
    outputs = attn_out.reshape(TOKEN_COUNT, HQ, HEAD_SIZE).astype(jnp.float32)
    row_delta = lax.optimization_barrier(jnp.sum(grad_heads * outputs, axis=2))
    keys_expanded = jnp.repeat(key_matrix.reshape(TOKEN_COUNT, KEY_VALUE_HEADS, HEAD_SIZE).astype(jnp.float32), QUERY_PER_KEY, axis=1)
    values_expanded = jnp.repeat(value_matrix.reshape(TOKEN_COUNT, KEY_VALUE_HEADS, HEAD_SIZE).astype(jnp.float32), QUERY_PER_KEY, axis=1)
    key_pos = jnp.arange(TOKEN_COUNT, dtype=jnp.int32)
    key_block = key_pos // BLK

    def tile_step(carried, block_index):
        key_running_total, value_running_total = carried
        row_start = block_index * BLK
        query_tile = lax.dynamic_slice_in_dim(queries, row_start, BLK, 0)
        grad_tile = lax.dynamic_slice_in_dim(grad_heads, row_start, BLK, 0)
        delta_tile = lax.dynamic_slice_in_dim(row_delta, row_start, BLK, 0)
        lse_tile = lax.dynamic_slice_in_dim(log_sums, row_start, BLK, 1)
        mask_row = lax.dynamic_index_in_dim(block_mask, block_index, 0, keepdims=False)
        allowed = mask_row[key_block]
        query_pos = row_start + jnp.arange(BLK, dtype=jnp.int32)
        earlier = ((key_block < block_index) & (allowed == 1))[None, :]
        diagonal = (key_block == block_index)[None, :] & (key_pos[None, :] <= query_pos[:, None])
        live_mask = earlier | diagonal
        scores = jnp.einsum('ihd,jhd->hij', query_tile, keys_expanded) * logit_scale
        probabilities = jnp.where(live_mask[None], jnp.exp(scores - lse_tile[:, :, None]), 0.0)
        prob_grad = jnp.einsum('ihd,jhd->hij', grad_tile, values_expanded)
        dscore = probabilities * (prob_grad - delta_tile.T[:, :, None])
        dscore = lax.optimization_barrier(dscore.astype(jnp.bfloat16)).astype(jnp.float32)
        rounded = lax.optimization_barrier(probabilities.astype(jnp.bfloat16)).astype(jnp.float32)
        query_term = jnp.einsum('hij,jhd->ihd', dscore, keys_expanded) * logit_scale
        key_running_total = key_running_total + jnp.einsum('hij,ihd->jhd', dscore, query_tile)
        value_running_total = value_running_total + jnp.einsum('hij,ihd->jhd', rounded, grad_tile)
        return ((key_running_total, value_running_total), query_term)
    zero_grad = jnp.zeros((TOKEN_COUNT, HQ, HEAD_SIZE), jnp.float32)
    (key_running_total, value_running_total), query_tiles = lax.scan(tile_step, (zero_grad, zero_grad), jnp.arange(NB, dtype=jnp.int32))
    query_grad = query_tiles.reshape(TOKEN_COUNT, HQ * HEAD_SIZE).astype(jnp.bfloat16)
    key_gradient_sum = lax.optimization_barrier(jnp.sum(key_running_total.reshape(TOKEN_COUNT, KEY_VALUE_HEADS, QUERY_PER_KEY, HEAD_SIZE), axis=2)) * logit_scale
    value_gradient_sum = lax.optimization_barrier(jnp.sum(value_running_total.reshape(TOKEN_COUNT, KEY_VALUE_HEADS, QUERY_PER_KEY, HEAD_SIZE), axis=2))
    key_gradient = key_gradient_sum.reshape(TOKEN_COUNT, KEY_VALUE_HEADS * HEAD_SIZE).astype(jnp.bfloat16)
    value_gradient = value_gradient_sum.reshape(TOKEN_COUNT, KEY_VALUE_HEADS * HEAD_SIZE).astype(jnp.bfloat16)
    return (query_grad, key_gradient, value_gradient)
```

```python
import math

import jax
import jax.numpy as jnp
from jax import lax
from jax.sharding import PartitionSpec as P

BLK = 128
HEAD_SIZE = 128


def live_region(block_mask, query_start, tok_rows, key_start, key_count):
    block_table = lax.dynamic_slice(
        block_mask, (query_start // BLK, key_start // BLK), (tok_rows // BLK, key_count // BLK)
    )
    block_table = jnp.repeat(jnp.repeat(block_table, BLK, axis=0), BLK, axis=1)
    query_pos = query_start + jnp.arange(tok_rows, dtype=jnp.int32)
    key_pos = key_start + jnp.arange(key_count, dtype=jnp.int32)
    query_block = (query_pos // BLK)[:, None]
    key_block = (key_pos // BLK)[None, :]
    earlier = (key_block < query_block) & (block_table == 1)
    diagonal = (key_block == query_block) & (key_pos[None, :] <= query_pos[:, None])
    return earlier | diagonal


def contract(queries, out_grads, row_delta, log_sums, keys_part, values_part, live_mask):
    logit_scale = 1.0 / math.sqrt(HEAD_SIZE)
    scores = (
        jnp.einsum("igd,jd->gij", queries, keys_part, preferred_element_type=jnp.float32)
        * logit_scale
    )
    probabilities = jnp.where(live_mask[None], jnp.exp(scores - log_sums[:, :, None]), 0.0)
    prob_grad = jnp.einsum(
        "igd,jd->gij", out_grads, values_part, preferred_element_type=jnp.float32
    )
    dscore = (probabilities * (prob_grad - row_delta[:, :, None])).astype(jnp.bfloat16)
    query_term = jnp.einsum("gij,jd->igd", dscore, keys_part, preferred_element_type=jnp.float32)
    key_term = jnp.einsum("gij,igd->jd", dscore, queries, preferred_element_type=jnp.float32)
    value_term = jnp.einsum(
        "gij,igd->jd",
        probabilities.astype(jnp.bfloat16),
        out_grads,
        preferred_element_type=jnp.float32,
    )
    return (query_term, key_term, value_term)


def local(query_rows, key_matrix, value_matrix, attn_out, out_grad, log_sums, block_mask):
    tok_rows = query_rows.shape[0]
    col_width = query_rows.shape[1]
    heads_local = col_width // HEAD_SIZE
    ctx_pos = lax.axis_index("ctx")
    ctx_count = lax.axis_size("ctx")
    tp_count = lax.axis_size("tp")
    grad_rows = out_grad.shape[0]
    pieces = out_grad.reshape(grad_rows, tp_count, col_width)
    own_grad = lax.all_to_all(pieces, "tp", split_axis=1, concat_axis=0, tiled=True)
    own_grad = own_grad.reshape(tok_rows, col_width)
    queries = query_rows.reshape(tok_rows, heads_local, HEAD_SIZE)
    out_grads = own_grad.reshape(tok_rows, heads_local, HEAD_SIZE)
    outputs = attn_out.reshape(tok_rows, heads_local, HEAD_SIZE)
    row_delta = jnp.sum(out_grads.astype(jnp.float32) * outputs.astype(jnp.float32), axis=2).T
    query_start = ctx_pos * tok_rows
    key_values = jnp.concatenate([key_matrix, value_matrix], axis=1)
    all_key_values = lax.all_gather(key_values, "ctx", axis=0, tiled=True)
    zero_query = jnp.zeros((tok_rows, heads_local, HEAD_SIZE), jnp.float32)
    zero_partial = jnp.zeros((ctx_count * tok_rows, 2 * HEAD_SIZE), jnp.float32)

    def visit_span(span, carried):
        query_acc, partial = carried
        key_start = span * tok_rows
        span_kv = lax.dynamic_slice_in_dim(all_key_values, key_start, tok_rows, 0)
        keys_part = span_kv[:, :HEAD_SIZE]
        values_part = span_kv[:, HEAD_SIZE:]
        live_mask = live_region(block_mask, query_start, tok_rows, key_start, tok_rows)
        query_term, key_term, value_term = contract(
            queries, out_grads, row_delta, log_sums, keys_part, values_part, live_mask
        )
        span_partial = jnp.concatenate([key_term, value_term], axis=1)
        partial = lax.dynamic_update_slice_in_dim(partial, span_partial, key_start, 0)
        return (query_acc + query_term, partial)

    query_acc, partial = lax.fori_loop(0, ctx_pos + 1, visit_span, (zero_query, zero_partial))
    summed = lax.psum_scatter(partial, "ctx", scatter_dimension=0, tiled=True)
    logit_scale = 1.0 / math.sqrt(HEAD_SIZE)
    query_grad = (query_acc * logit_scale).reshape(tok_rows, col_width).astype(jnp.bfloat16)
    key_gradient = (summed[:, :HEAD_SIZE] * logit_scale).astype(jnp.bfloat16)
    value_gradient = summed[:, HEAD_SIZE:].astype(jnp.bfloat16)
    return (query_grad, key_gradient, value_gradient)


def solution(mesh):
    placed = (
        P(("dp", "ctx"), "tp"),
        P(("dp", "ctx"), "tp"),
        P(("dp", "ctx"), "tp"),
        P(("dp", "ctx"), "tp"),
        P(("dp", "ctx", "tp"), None),
        P("tp", ("dp", "ctx")),
        P("dp", None),
    )
    return jax.shard_map(
        local,
        mesh=mesh,
        in_specs=placed,
        out_specs=(P(("dp", "ctx"), "tp"), P(("dp", "ctx"), "tp"), P(("dp", "ctx"), "tp")),
        check_vma=False,
    )
```

```python
import math

import jax
import jax.numpy as jnp
from jax import lax
from jax.sharding import PartitionSpec as P

BLK = 128
HEAD_SIZE = 128
Y_HI = 2


def ring_of(ctx_count):
    half = ctx_count // Y_HI
    return [Y_HI * p if p < half else Y_HI * (ctx_count - 1 - p) + 1 for p in range(ctx_count)]


def ring_index(ctx_pos, ctx_count):
    half = ctx_count // Y_HI
    z = ctx_pos // Y_HI
    return jnp.where(ctx_pos % Y_HI == 0, z, ctx_count - 1 - z)


def owner_of(ring_pos, ctx_count):
    half = ctx_count // Y_HI
    return jnp.where(ring_pos < half, Y_HI * ring_pos, Y_HI * (ctx_count - 1 - ring_pos) + 1)


def from_ahead(value, ctx_count):
    order = ring_of(ctx_count)
    pairs = [(order[p], order[(p - 1) % ctx_count]) for p in range(ctx_count)]
    return lax.ppermute(value, "ctx", pairs)


def live_region(block_mask, query_start, tok_rows, key_start, key_count):
    block_table = lax.dynamic_slice(
        block_mask, (query_start // BLK, key_start // BLK), (tok_rows // BLK, key_count // BLK)
    )
    block_table = jnp.repeat(jnp.repeat(block_table, BLK, axis=0), BLK, axis=1)
    query_pos = query_start + jnp.arange(tok_rows, dtype=jnp.int32)
    key_pos = key_start + jnp.arange(key_count, dtype=jnp.int32)
    query_block = (query_pos // BLK)[:, None]
    key_block = (key_pos // BLK)[None, :]
    earlier = (key_block < query_block) & (block_table == 1)
    diagonal = (key_block == query_block) & (key_pos[None, :] <= query_pos[:, None])
    return earlier | diagonal


def contract(queries, out_grads, row_delta, log_sums, keys_part, values_part, live_mask):
    logit_scale = 1.0 / math.sqrt(HEAD_SIZE)
    scores = (
        jnp.einsum("igd,jd->gij", queries, keys_part, preferred_element_type=jnp.float32)
        * logit_scale
    )
    probabilities = jnp.where(live_mask[None], jnp.exp(scores - log_sums[:, :, None]), 0.0)
    prob_grad = jnp.einsum(
        "igd,jd->gij", out_grads, values_part, preferred_element_type=jnp.float32
    )
    dscore = (probabilities * (prob_grad - row_delta[:, :, None])).astype(jnp.bfloat16)
    query_term = jnp.einsum("gij,jd->igd", dscore, keys_part, preferred_element_type=jnp.float32)
    key_term = jnp.einsum("gij,igd->jd", dscore, queries, preferred_element_type=jnp.float32)
    value_term = jnp.einsum(
        "gij,igd->jd",
        probabilities.astype(jnp.bfloat16),
        out_grads,
        preferred_element_type=jnp.float32,
    )
    return (query_term, key_term, value_term)


def local(query_rows, key_matrix, value_matrix, attn_out, out_grad, log_sums, block_mask):
    tok_rows = query_rows.shape[0]
    col_width = query_rows.shape[1]
    heads_local = col_width // HEAD_SIZE
    ctx_pos = lax.axis_index("ctx")
    ctx_count = lax.axis_size("ctx")
    tp_count = lax.axis_size("tp")
    grad_rows = out_grad.shape[0]
    pieces = out_grad.reshape(grad_rows, tp_count, col_width)
    own_grad = lax.all_to_all(pieces, "tp", split_axis=1, concat_axis=0, tiled=True)
    queries = query_rows.reshape(tok_rows, heads_local, HEAD_SIZE)
    out_grads = own_grad.reshape(tok_rows, heads_local, HEAD_SIZE)
    outputs = attn_out.reshape(tok_rows, heads_local, HEAD_SIZE)
    row_delta = jnp.sum(out_grads.astype(jnp.float32) * outputs.astype(jnp.float32), axis=2).T
    query_start = ctx_pos * tok_rows
    ring_pos = ring_index(ctx_pos, ctx_count)

    def terms(key_values, turn):
        owner = owner_of((ring_pos + turn) % ctx_count, ctx_count)
        key_start = owner * tok_rows
        live_mask = live_region(block_mask, query_start, tok_rows, key_start, tok_rows)
        query_term, key_term, value_term = contract(
            queries,
            out_grads,
            row_delta,
            log_sums,
            key_values[:, :HEAD_SIZE],
            key_values[:, HEAD_SIZE:],
            live_mask,
        )
        return query_term, jnp.concatenate([key_term, value_term], axis=1)

    key_values = jnp.concatenate([key_matrix, value_matrix], axis=1)
    next_kv = from_ahead(key_values, ctx_count)
    query_acc, pending = terms(key_values, 0)

    def visit_turn(turn, carried):
        key_values, query_acc, pending = carried
        received = from_ahead(pending, ctx_count)
        next_kv = from_ahead(key_values, ctx_count)
        query_term, kv_term = terms(key_values, turn)
        return (next_kv, query_acc + query_term, received + kv_term)

    key_values, query_acc, pending = lax.fori_loop(
        1, ctx_count - 1, visit_turn, (next_kv, query_acc, pending)
    )
    received = from_ahead(pending, ctx_count)
    query_term, kv_term = terms(key_values, ctx_count - 1)
    query_acc = query_acc + query_term
    summed = from_ahead(received + kv_term, ctx_count)
    logit_scale = 1.0 / math.sqrt(HEAD_SIZE)
    query_grad = (query_acc * logit_scale).reshape(tok_rows, col_width).astype(jnp.bfloat16)
    key_gradient = (summed[:, :HEAD_SIZE] * logit_scale).astype(jnp.bfloat16)
    value_gradient = summed[:, HEAD_SIZE:].astype(jnp.bfloat16)
    return (query_grad, key_gradient, value_gradient)


def solution(mesh):
    placed = (
        P(("dp", "ctx"), "tp"),
        P(("dp", "ctx"), "tp"),
        P(("dp", "ctx"), "tp"),
        P(("dp", "ctx"), "tp"),
        P(("dp", "ctx", "tp"), None),
        P("tp", ("dp", "ctx")),
        P("dp", None),
    )
    return jax.shard_map(
        local,
        mesh=mesh,
        in_specs=placed,
        out_specs=(P(("dp", "ctx"), "tp"), P(("dp", "ctx"), "tp"), P(("dp", "ctx"), "tp")),
        check_vma=False,
    )
```

```python
import math

import jax
import jax.numpy as jnp
from jax import lax
from jax.sharding import PartitionSpec as P

BLK = 128
HEAD_SIZE = 128
Y_HI = 2


def ring_of(ctx_count):
    half = ctx_count // Y_HI
    return [Y_HI * p if p < half else Y_HI * (ctx_count - 1 - p) + 1 for p in range(ctx_count)]


def ring_index(ctx_pos, ctx_count):
    half = ctx_count // Y_HI
    z = ctx_pos // Y_HI
    return jnp.where(ctx_pos % Y_HI == 0, z, ctx_count - 1 - z)


def owner_of(ring_pos, ctx_count):
    half = ctx_count // Y_HI
    return jnp.where(ring_pos < half, Y_HI * ring_pos, Y_HI * (ctx_count - 1 - ring_pos) + 1)


def from_ahead(value, ctx_count):
    order = ring_of(ctx_count)
    pairs = [(order[p], order[(p - 1) % ctx_count]) for p in range(ctx_count)]
    return lax.ppermute(value, "ctx", pairs)


def from_behind(value, ctx_count):
    order = ring_of(ctx_count)
    pairs = [(order[p], order[(p + 1) % ctx_count]) for p in range(ctx_count)]
    return lax.ppermute(value, "ctx", pairs)


def live_region(block_mask, query_start, tok_rows, key_pos):
    query_rows = lax.dynamic_slice_in_dim(block_mask, query_start // BLK, tok_rows // BLK, 0)
    block_table = jnp.take(query_rows, key_pos[::BLK] // BLK, axis=1)
    block_table = jnp.repeat(jnp.repeat(block_table, BLK, axis=0), BLK, axis=1)
    query_pos = query_start + jnp.arange(tok_rows, dtype=jnp.int32)
    query_block = (query_pos // BLK)[:, None]
    key_block = (key_pos // BLK)[None, :]
    earlier = (key_block < query_block) & (block_table == 1)
    diagonal = (key_block == query_block) & (key_pos[None, :] <= query_pos[:, None])
    return earlier | diagonal


def contract(queries, out_grads, row_delta, log_sums, keys_part, values_part, live_mask):
    logit_scale = 1.0 / math.sqrt(HEAD_SIZE)
    scores = (
        jnp.einsum("igd,jd->gij", queries, keys_part, preferred_element_type=jnp.float32)
        * logit_scale
    )
    probabilities = jnp.where(live_mask[None], jnp.exp(scores - log_sums[:, :, None]), 0.0)
    prob_grad = jnp.einsum(
        "igd,jd->gij", out_grads, values_part, preferred_element_type=jnp.float32
    )
    dscore = (probabilities * (prob_grad - row_delta[:, :, None])).astype(jnp.bfloat16)
    query_term = jnp.einsum("gij,jd->igd", dscore, keys_part, preferred_element_type=jnp.float32)
    key_term = jnp.einsum("gij,igd->jd", dscore, queries, preferred_element_type=jnp.float32)
    value_term = jnp.einsum(
        "gij,igd->jd",
        probabilities.astype(jnp.bfloat16),
        out_grads,
        preferred_element_type=jnp.float32,
    )
    return (query_term, key_term, value_term)


def local(query_rows, key_matrix, value_matrix, attn_out, out_grad, log_sums, block_mask):
    tok_rows = query_rows.shape[0]
    col_width = query_rows.shape[1]
    heads_local = col_width // HEAD_SIZE
    ctx_pos = lax.axis_index("ctx")
    ctx_count = lax.axis_size("ctx")
    tp_count = lax.axis_size("tp")
    grad_rows = out_grad.shape[0]
    pieces = out_grad.reshape(grad_rows, tp_count, col_width)
    own_grad = lax.all_to_all(pieces, "tp", split_axis=1, concat_axis=0, tiled=True)
    queries = query_rows.reshape(tok_rows, heads_local, HEAD_SIZE)
    out_grads = own_grad.reshape(tok_rows, heads_local, HEAD_SIZE)
    outputs = attn_out.reshape(tok_rows, heads_local, HEAD_SIZE)
    row_delta = jnp.sum(out_grads.astype(jnp.float32) * outputs.astype(jnp.float32), axis=2).T
    query_start = ctx_pos * tok_rows
    ring_pos = ring_index(ctx_pos, ctx_count)

    half = tok_rows // 2
    offsets = jnp.arange(half, dtype=jnp.int32)

    def terms(ahead_kv, behind_kv, turn):
        ahead_owner = owner_of((ring_pos + turn) % ctx_count, ctx_count)
        behind_owner = owner_of((ring_pos - turn) % ctx_count, ctx_count)
        key_pos = jnp.concatenate(
            [ahead_owner * tok_rows + offsets, behind_owner * tok_rows + half + offsets]
        )
        live_mask = live_region(block_mask, query_start, tok_rows, key_pos)
        key_values = jnp.concatenate([ahead_kv, behind_kv], axis=0)
        query_term, key_term, value_term = contract(
            queries,
            out_grads,
            row_delta,
            log_sums,
            key_values[:, :HEAD_SIZE],
            key_values[:, HEAD_SIZE:],
            live_mask,
        )
        kv_term = jnp.concatenate([key_term, value_term], axis=1)
        return query_term, kv_term[:half], kv_term[half:]

    key_values = jnp.concatenate([key_matrix, value_matrix], axis=1)
    ahead_kv = key_values[:half]
    behind_kv = key_values[half:]
    next_ahead = from_ahead(ahead_kv, ctx_count)
    next_behind = from_behind(behind_kv, ctx_count)
    query_acc, ahead_pending, behind_pending = terms(ahead_kv, behind_kv, 0)

    def visit_turn(turn, carried):
        ahead_kv, behind_kv, query_acc, ahead_pending, behind_pending = carried
        ahead_received = from_ahead(ahead_pending, ctx_count)
        behind_received = from_behind(behind_pending, ctx_count)
        next_ahead = from_ahead(ahead_kv, ctx_count)
        next_behind = from_behind(behind_kv, ctx_count)
        query_term, ahead_term, behind_term = terms(ahead_kv, behind_kv, turn)
        return (
            next_ahead,
            next_behind,
            query_acc + query_term,
            ahead_received + ahead_term,
            behind_received + behind_term,
        )

    ahead_kv, behind_kv, query_acc, ahead_pending, behind_pending = lax.fori_loop(
        1,
        ctx_count - 1,
        visit_turn,
        (next_ahead, next_behind, query_acc, ahead_pending, behind_pending),
    )
    ahead_received = from_ahead(ahead_pending, ctx_count)
    behind_received = from_behind(behind_pending, ctx_count)
    query_term, ahead_term, behind_term = terms(ahead_kv, behind_kv, ctx_count - 1)
    query_acc = query_acc + query_term
    summed = jnp.concatenate(
        [
            from_ahead(ahead_received + ahead_term, ctx_count),
            from_behind(behind_received + behind_term, ctx_count),
        ],
        axis=0,
    )
    logit_scale = 1.0 / math.sqrt(HEAD_SIZE)
    query_grad = (query_acc * logit_scale).reshape(tok_rows, col_width).astype(jnp.bfloat16)
    key_gradient = (summed[:, :HEAD_SIZE] * logit_scale).astype(jnp.bfloat16)
    value_gradient = summed[:, HEAD_SIZE:].astype(jnp.bfloat16)
    return (query_grad, key_gradient, value_gradient)


def solution(mesh):
    placed = (
        P(("dp", "ctx"), "tp"),
        P(("dp", "ctx"), "tp"),
        P(("dp", "ctx"), "tp"),
        P(("dp", "ctx"), "tp"),
        P(("dp", "ctx", "tp"), None),
        P("tp", ("dp", "ctx")),
        P("dp", None),
    )
    return jax.shard_map(
        local,
        mesh=mesh,
        in_specs=placed,
        out_specs=(P(("dp", "ctx"), "tp"), P(("dp", "ctx"), "tp"), P(("dp", "ctx"), "tp")),
        check_vma=False,
    )
```

```python
import math

import jax
import jax.numpy as jnp
from jax import lax
from jax.sharding import PartitionSpec as P

BLK = 128
HEAD_SIZE = 128
Y_HI = 2


def along_z(value, ctx_count, shift):
    z_count = ctx_count // Y_HI
    pairs = [
        (Y_HI * ((z + shift) % z_count) + h, Y_HI * z + h)
        for z in range(z_count)
        for h in range(Y_HI)
    ]
    return lax.ppermute(value, "ctx", pairs)


def from_partner(value, ctx_count):
    pairs = [(c, c ^ 1) for c in range(ctx_count)]
    return lax.ppermute(value, "ctx", pairs)


def live_region(block_mask, query_start, tok_rows, key_pos):
    query_rows = lax.dynamic_slice_in_dim(block_mask, query_start // BLK, tok_rows // BLK, 0)
    block_table = jnp.take(query_rows, key_pos[::BLK] // BLK, axis=1)
    block_table = jnp.repeat(jnp.repeat(block_table, BLK, axis=0), BLK, axis=1)
    query_pos = query_start + jnp.arange(tok_rows, dtype=jnp.int32)
    query_block = (query_pos // BLK)[:, None]
    key_block = (key_pos // BLK)[None, :]
    earlier = (key_block < query_block) & (block_table == 1)
    diagonal = (key_block == query_block) & (key_pos[None, :] <= query_pos[:, None])
    return earlier | diagonal


def contract(queries, out_grads, row_delta, log_sums, keys_part, values_part, live_mask):
    logit_scale = 1.0 / math.sqrt(HEAD_SIZE)
    scores = (
        jnp.einsum("igd,jd->gij", queries, keys_part, preferred_element_type=jnp.float32)
        * logit_scale
    )
    probabilities = jnp.where(live_mask[None], jnp.exp(scores - log_sums[:, :, None]), 0.0)
    prob_grad = jnp.einsum(
        "igd,jd->gij", out_grads, values_part, preferred_element_type=jnp.float32
    )
    dscore = (probabilities * (prob_grad - row_delta[:, :, None])).astype(jnp.bfloat16)
    query_term = jnp.einsum("gij,jd->igd", dscore, keys_part, preferred_element_type=jnp.float32)
    key_term = jnp.einsum("gij,igd->jd", dscore, queries, preferred_element_type=jnp.float32)
    value_term = jnp.einsum(
        "gij,igd->jd",
        probabilities.astype(jnp.bfloat16),
        out_grads,
        preferred_element_type=jnp.float32,
    )
    return (query_term, key_term, value_term)


def local(query_rows, key_matrix, value_matrix, attn_out, out_grad, log_sums, block_mask):
    tok_rows = query_rows.shape[0]
    col_width = query_rows.shape[1]
    heads_local = col_width // HEAD_SIZE
    ctx_pos = lax.axis_index("ctx")
    ctx_count = lax.axis_size("ctx")
    tp_count = lax.axis_size("tp")
    grad_rows = out_grad.shape[0]
    pieces = out_grad.reshape(grad_rows, tp_count, col_width)
    own_grad = lax.all_to_all(pieces, "tp", split_axis=1, concat_axis=0, tiled=True)
    queries = query_rows.reshape(tok_rows, heads_local, HEAD_SIZE)
    out_grads = own_grad.reshape(tok_rows, heads_local, HEAD_SIZE)
    outputs = attn_out.reshape(tok_rows, heads_local, HEAD_SIZE)
    row_delta = jnp.sum(out_grads.astype(jnp.float32) * outputs.astype(jnp.float32), axis=2).T
    query_start = ctx_pos * tok_rows
    z_pos = ctx_pos // Y_HI
    z_count = ctx_count // Y_HI
    y_hi = ctx_pos % Y_HI
    super_rows = Y_HI * tok_rows
    offsets = jnp.arange(tok_rows, dtype=jnp.int32)

    def terms(ahead_kv, behind_kv, turn):
        ahead_owner = (z_pos + turn) % z_count
        behind_owner = (z_pos - turn) % z_count
        key_pos = jnp.concatenate(
            [ahead_owner * super_rows + offsets, behind_owner * super_rows + tok_rows + offsets]
        )
        live_mask = live_region(block_mask, query_start, tok_rows, key_pos)
        key_values = jnp.concatenate([ahead_kv, behind_kv], axis=0)
        query_term, key_term, value_term = contract(
            queries,
            out_grads,
            row_delta,
            log_sums,
            key_values[:, :HEAD_SIZE],
            key_values[:, HEAD_SIZE:],
            live_mask,
        )
        kv_term = jnp.concatenate([key_term, value_term], axis=1)
        return query_term, kv_term[:tok_rows], kv_term[tok_rows:]

    key_values = jnp.concatenate([key_matrix, value_matrix], axis=1)
    partner_kv = from_partner(key_values, ctx_count)
    ahead_kv = jnp.where(y_hi == 0, key_values, partner_kv)
    behind_kv = jnp.where(y_hi == 0, partner_kv, key_values)
    next_ahead = along_z(ahead_kv, ctx_count, 1)
    next_behind = along_z(behind_kv, ctx_count, -1)
    query_acc, ahead_pending, behind_pending = terms(ahead_kv, behind_kv, 0)

    def visit_turn(turn, carried):
        ahead_kv, behind_kv, query_acc, ahead_pending, behind_pending = carried
        ahead_received = along_z(ahead_pending, ctx_count, 1)
        behind_received = along_z(behind_pending, ctx_count, -1)
        next_ahead = along_z(ahead_kv, ctx_count, 1)
        next_behind = along_z(behind_kv, ctx_count, -1)
        query_term, ahead_term, behind_term = terms(ahead_kv, behind_kv, turn)
        return (
            next_ahead,
            next_behind,
            query_acc + query_term,
            ahead_received + ahead_term,
            behind_received + behind_term,
        )

    ahead_kv, behind_kv, query_acc, ahead_pending, behind_pending = lax.fori_loop(
        1,
        z_count - 1,
        visit_turn,
        (next_ahead, next_behind, query_acc, ahead_pending, behind_pending),
    )
    ahead_received = along_z(ahead_pending, ctx_count, 1)
    behind_received = along_z(behind_pending, ctx_count, -1)
    query_term, ahead_term, behind_term = terms(ahead_kv, behind_kv, z_count - 1)
    query_acc = query_acc + query_term
    ahead_total = along_z(ahead_received + ahead_term, ctx_count, 1)
    behind_total = along_z(behind_received + behind_term, ctx_count, -1)
    own_total = jnp.where(y_hi == 0, ahead_total, behind_total)
    other_total = jnp.where(y_hi == 0, behind_total, ahead_total)
    summed = own_total + from_partner(other_total, ctx_count)
    logit_scale = 1.0 / math.sqrt(HEAD_SIZE)
    query_grad = (query_acc * logit_scale).reshape(tok_rows, col_width).astype(jnp.bfloat16)
    key_gradient = (summed[:, :HEAD_SIZE] * logit_scale).astype(jnp.bfloat16)
    value_gradient = summed[:, HEAD_SIZE:].astype(jnp.bfloat16)
    return (query_grad, key_gradient, value_gradient)


def solution(mesh):
    placed = (
        P(("dp", "ctx"), "tp"),
        P(("dp", "ctx"), "tp"),
        P(("dp", "ctx"), "tp"),
        P(("dp", "ctx"), "tp"),
        P(("dp", "ctx", "tp"), None),
        P("tp", ("dp", "ctx")),
        P("dp", None),
    )
    return jax.shard_map(
        local,
        mesh=mesh,
        in_specs=placed,
        out_specs=(P(("dp", "ctx"), "tp"), P(("dp", "ctx"), "tp"), P(("dp", "ctx"), "tp")),
        check_vma=False,
    )
```

```python
import math

import jax
import jax.numpy as jnp
from jax import lax
from jax.experimental import pallas as pl
from jax.experimental.pallas import tpu as pltpu
from jax.sharding import PartitionSpec as P

BLK = 128
HEAD_SIZE = 128
Y_HI = 2


def along_z(value, ctx_count, shift):
    z_count = ctx_count // Y_HI
    pairs = [
        (Y_HI * ((z + shift) % z_count) + h, Y_HI * z + h)
        for z in range(z_count)
        for h in range(Y_HI)
    ]
    return lax.ppermute(value, "ctx", pairs)


def from_partner(value, ctx_count):
    pairs = [(c, c ^ 1) for c in range(ctx_count)]
    return lax.ppermute(value, "ctx", pairs)


def turn_kernel(info_ref, q_ref, do_ref, kv_ref, lse_ref, delta_ref, dq_in_ref, dq_ref, dkdv_ref):
    tok_rows = q_ref.shape[0]
    key_count = kv_ref.shape[0]
    heads = q_ref.shape[1] // HEAD_SIZE
    scale = 1.0 / math.sqrt(HEAD_SIZE)
    row = lax.broadcasted_iota(jnp.int32, (tok_rows, key_count), 0)
    row_block = row // BLK
    flags = info_ref[0:1, :]
    for r in range(1, tok_rows // BLK):
        flags = jnp.where(row_block == r, info_ref[r : r + 1, :], flags)
    nb = tok_rows // BLK
    diag = (info_ref[nb : nb + 1, :] == row_block) & (info_ref[nb + 1 : nb + 2, :] <= row)
    live = (flags == 1) | diag
    keys = kv_ref[:, :HEAD_SIZE]
    values = kv_ref[:, HEAD_SIZE:]
    dk = jnp.zeros((key_count, HEAD_SIZE), jnp.float32)
    dv = jnp.zeros((key_count, HEAD_SIZE), jnp.float32)
    for h in range(heads):
        cols = slice(h * HEAD_SIZE, (h + 1) * HEAD_SIZE)
        q = q_ref[:, cols]
        do = do_ref[:, cols]
        s = lax.dot_general(q, keys, (((1,), (1,)), ((), ())), preferred_element_type=jnp.float32)
        p = jnp.where(live, jnp.exp(s * scale - lse_ref[:, h : h + 1]), 0.0)
        dp = lax.dot_general(do, values, (((1,), (1,)), ((), ())), preferred_element_type=jnp.float32)
        ds = (p * (dp - delta_ref[:, h : h + 1])).astype(jnp.bfloat16).astype(keys.dtype)
        dq_ref[:, cols] = dq_in_ref[:, cols] + jnp.dot(ds, keys, preferred_element_type=jnp.float32)
        dk = dk + lax.dot_general(ds, q, (((0,), (0,)), ((), ())), preferred_element_type=jnp.float32)
        dv = dv + lax.dot_general(
            p.astype(jnp.bfloat16).astype(do.dtype), do, (((0,), (0,)), ((), ())), preferred_element_type=jnp.float32
        )
    dkdv_ref[:, :HEAD_SIZE] = dk
    dkdv_ref[:, HEAD_SIZE:] = dv


def turn_call(info, q, do, kv, lse_t, delta_t, dq_acc):
    tok_rows, width = q.shape
    key_count = kv.shape[0]
    spec = pl.BlockSpec(memory_space=pltpu.MemorySpace.VMEM)
    return pl.pallas_call(
        turn_kernel,
        out_shape=(
            jax.ShapeDtypeStruct((tok_rows, width), jnp.float32),
            jax.ShapeDtypeStruct((key_count, 2 * HEAD_SIZE), jnp.float32),
        ),
        in_specs=[spec] * 7,
        out_specs=(spec, spec),
        input_output_aliases={6: 0},
    )(info, q, do, kv, lse_t, delta_t, dq_acc)


def local(query_rows, key_matrix, value_matrix, attn_out, out_grad, log_sums, block_mask):
    tok_rows = query_rows.shape[0]
    col_width = query_rows.shape[1]
    heads_local = col_width // HEAD_SIZE
    ctx_pos = lax.axis_index("ctx")
    ctx_count = lax.axis_size("ctx")
    tp_count = lax.axis_size("tp")
    grad_rows = out_grad.shape[0]
    pieces = out_grad.reshape(grad_rows, tp_count, col_width)
    own_grad = lax.all_to_all(pieces, "tp", split_axis=1, concat_axis=0, tiled=True)
    own_grad = own_grad.reshape(tok_rows, col_width)
    out_grads = own_grad.reshape(tok_rows, heads_local, HEAD_SIZE)
    outputs = attn_out.reshape(tok_rows, heads_local, HEAD_SIZE)
    delta_t = jnp.sum(out_grads.astype(jnp.float32) * outputs.astype(jnp.float32), axis=2)
    lse_t = log_sums.T
    query_start = ctx_pos * tok_rows
    z_pos = ctx_pos // Y_HI
    z_count = ctx_count // Y_HI
    y_hi = ctx_pos % Y_HI
    super_rows = Y_HI * tok_rows
    offsets = jnp.arange(tok_rows, dtype=jnp.int32)

    def terms(ahead_kv, behind_kv, turn, query_acc):
        ahead_owner = (z_pos + turn) % z_count
        behind_owner = (z_pos - turn) % z_count
        key_pos = jnp.concatenate(
            [ahead_owner * super_rows + offsets, behind_owner * super_rows + tok_rows + offsets]
        )
        key_block = key_pos // BLK
        query_block = query_start // BLK + jnp.arange(tok_rows // BLK, dtype=jnp.int32)
        mask_rows = lax.dynamic_slice_in_dim(block_mask, query_start // BLK, tok_rows // BLK, 0)
        allowed = jnp.take(mask_rows, key_block, axis=1)
        flags = (key_block[None, :] < query_block[:, None]) & (allowed == 1)
        info = jnp.concatenate(
            [
                flags.astype(jnp.int32),
                (key_block - query_start // BLK)[None, :],
                (key_pos - query_start)[None, :],
            ],
            axis=0,
        )
        key_values = jnp.concatenate([ahead_kv, behind_kv], axis=0)
        query_acc, kv_term = turn_call(
            info, query_rows, own_grad, key_values, lse_t, delta_t, query_acc
        )
        return query_acc, kv_term[:tok_rows], kv_term[tok_rows:]

    key_values = jnp.concatenate([key_matrix, value_matrix], axis=1)
    partner_kv = from_partner(key_values, ctx_count)
    ahead_kv = jnp.where(y_hi == 0, key_values, partner_kv)
    behind_kv = jnp.where(y_hi == 0, partner_kv, key_values)
    next_ahead = along_z(ahead_kv, ctx_count, 1)
    next_behind = along_z(behind_kv, ctx_count, -1)
    zero_query = jnp.zeros((tok_rows, col_width), jnp.float32)
    query_acc, ahead_pending, behind_pending = terms(ahead_kv, behind_kv, 0, zero_query)

    def visit_turn(turn, carried):
        ahead_kv, behind_kv, query_acc, ahead_pending, behind_pending = carried
        ahead_received = along_z(ahead_pending, ctx_count, 1)
        behind_received = along_z(behind_pending, ctx_count, -1)
        next_ahead = along_z(ahead_kv, ctx_count, 1)
        next_behind = along_z(behind_kv, ctx_count, -1)
        query_acc, ahead_term, behind_term = terms(ahead_kv, behind_kv, turn, query_acc)
        return (
            next_ahead,
            next_behind,
            query_acc,
            ahead_received + ahead_term,
            behind_received + behind_term,
        )

    ahead_kv, behind_kv, query_acc, ahead_pending, behind_pending = lax.fori_loop(
        1,
        z_count - 1,
        visit_turn,
        (next_ahead, next_behind, query_acc, ahead_pending, behind_pending),
    )
    ahead_received = along_z(ahead_pending, ctx_count, 1)
    behind_received = along_z(behind_pending, ctx_count, -1)
    query_acc, ahead_term, behind_term = terms(ahead_kv, behind_kv, z_count - 1, query_acc)
    ahead_total = along_z(ahead_received + ahead_term, ctx_count, 1)
    behind_total = along_z(behind_received + behind_term, ctx_count, -1)
    own_total = jnp.where(y_hi == 0, ahead_total, behind_total)
    other_total = jnp.where(y_hi == 0, behind_total, ahead_total)
    summed = own_total + from_partner(other_total, ctx_count)
    logit_scale = 1.0 / math.sqrt(HEAD_SIZE)
    query_grad = (query_acc * logit_scale).astype(jnp.bfloat16)
    key_gradient = (summed[:, :HEAD_SIZE] * logit_scale).astype(jnp.bfloat16)
    value_gradient = summed[:, HEAD_SIZE:].astype(jnp.bfloat16)
    return (query_grad, key_gradient, value_gradient)


def solution(mesh):
    placed = (
        P(("dp", "ctx"), "tp"),
        P(("dp", "ctx"), "tp"),
        P(("dp", "ctx"), "tp"),
        P(("dp", "ctx"), "tp"),
        P(("dp", "ctx", "tp"), None),
        P("tp", ("dp", "ctx")),
        P("dp", None),
    )
    return jax.shard_map(
        local,
        mesh=mesh,
        in_specs=placed,
        out_specs=(P(("dp", "ctx"), "tp"), P(("dp", "ctx"), "tp"), P(("dp", "ctx"), "tp")),
        check_vma=False,
    )
```

```python
import math

import jax
import jax.numpy as jnp
from jax import lax
from jax.experimental import pallas as pl
from jax.experimental.pallas import tpu as pltpu
from jax.sharding import PartitionSpec as P

BLK = 128
HEAD_SIZE = 128
Y_HI = 2


def along_z(value, ctx_count, shift):
    z_count = ctx_count // Y_HI
    pairs = [
        (Y_HI * ((z + shift) % z_count) + h, Y_HI * z + h)
        for z in range(z_count)
        for h in range(Y_HI)
    ]
    return lax.ppermute(value, "ctx", pairs)


def from_partner(value, ctx_count):
    pairs = [(c, c ^ 1) for c in range(ctx_count)]
    return lax.ppermute(value, "ctx", pairs)


def turn_kernel(turn_ref, code_ref, q_ref, do_ref, ahead_kv_ref, behind_kv_ref, lse_ref, delta_ref, dq_in_ref,
                dq_ref, ahead_ref, behind_ref):
    heads, tok_rows, _ = q_ref.shape
    key_count = 2 * ahead_kv_ref.shape[0]
    row_blocks = tok_rows // BLK
    key_blocks = key_count // BLK
    half_blocks = key_blocks // 2
    scale = 1.0 / math.sqrt(HEAD_SIZE)
    turn = turn_ref[0]
    codes = [[code_ref[turn, r * key_blocks + c] for c in range(key_blocks)] for r in range(row_blocks)]
    ahead_ref[...] = jnp.zeros(ahead_ref.shape, jnp.float32)
    behind_ref[...] = jnp.zeros(behind_ref.shape, jnp.float32)
    row = lax.broadcasted_iota(jnp.int32, (tok_rows, BLK), 0)
    col = lax.broadcasted_iota(jnp.int32, (tok_rows, BLK), 1)
    row_block = row // BLK
    below = col <= row - row_block * BLK

    def head_body(h, carry):
        q = q_ref[h]
        do = do_ref[h]
        lse = lse_ref[h]
        delta = delta_ref[h]
        dq_ref[h] = dq_in_ref[h]
        for c in range(key_blocks):
            any_live = codes[0][c] > 0
            for r in range(1, row_blocks):
                any_live = any_live | (codes[r][c] > 0)

            @pl.when(any_live)
            def _():
                code = jnp.full((tok_rows, BLK), codes[0][c], jnp.int32)
                for r in range(1, row_blocks):
                    code = jnp.where(row_block == r, codes[r][c], code)
                live = (code == 1) | ((code == 2) & below)
                kv_ref = ahead_kv_ref if c < half_blocks else behind_kv_ref
                rows = slice((c % half_blocks) * BLK, (c % half_blocks + 1) * BLK)
                keys = kv_ref[rows, :HEAD_SIZE]
                values = kv_ref[rows, HEAD_SIZE:]
                s = lax.dot_general(q, keys, (((1,), (1,)), ((), ())), preferred_element_type=jnp.float32)
                p = jnp.where(live, jnp.exp(s * scale - lse), 0.0)
                dp = lax.dot_general(do, values, (((1,), (1,)), ((), ())), preferred_element_type=jnp.float32)
                ds = (p * (dp - delta)).astype(jnp.bfloat16).astype(keys.dtype)
                dq_ref[h] = dq_ref[h] + jnp.dot(ds, keys, preferred_element_type=jnp.float32)
                dk = lax.dot_general(ds, q, (((0,), (0,)), ((), ())), preferred_element_type=jnp.float32)
                dv = lax.dot_general(
                    p.astype(jnp.bfloat16).astype(do.dtype), do, (((0,), (0,)), ((), ())),
                    preferred_element_type=jnp.float32,
                )
                out = ahead_ref if c < half_blocks else behind_ref
                out[rows, :HEAD_SIZE] = out[rows, :HEAD_SIZE] + dk
                out[rows, HEAD_SIZE:] = out[rows, HEAD_SIZE:] + dv

        return carry

    lax.fori_loop(0, heads, head_body, 0)


def turn_call(turn, codes, q, do, ahead_kv, behind_kv, lse, delta, dq_acc):
    heads, tok_rows, _ = q.shape
    half = ahead_kv.shape[0]
    vmem = pl.BlockSpec(memory_space=pltpu.MemorySpace.VMEM)
    smem = pl.BlockSpec(memory_space=pltpu.MemorySpace.SMEM)
    return pl.pallas_call(
        turn_kernel,
        out_shape=(
            jax.ShapeDtypeStruct(dq_acc.shape, jnp.float32),
            jax.ShapeDtypeStruct((half, 2 * HEAD_SIZE), jnp.float32),
            jax.ShapeDtypeStruct((half, 2 * HEAD_SIZE), jnp.float32),
        ),
        in_specs=[smem, smem] + [vmem] * 7,
        out_specs=(vmem, vmem, vmem),
        input_output_aliases={8: 0},
    )(turn, codes, q, do, ahead_kv, behind_kv, lse, delta, dq_acc)


def local(query_rows, key_matrix, value_matrix, attn_out, out_grad, log_sums, block_mask):
    tok_rows = query_rows.shape[0]
    col_width = query_rows.shape[1]
    heads_local = col_width // HEAD_SIZE
    ctx_pos = lax.axis_index("ctx")
    ctx_count = lax.axis_size("ctx")
    tp_count = lax.axis_size("tp")
    grad_rows = out_grad.shape[0]
    pieces = out_grad.reshape(grad_rows, tp_count, col_width)
    own_grad = lax.all_to_all(pieces, "tp", split_axis=1, concat_axis=0, tiled=True)
    out_grads = own_grad.reshape(tok_rows, heads_local, HEAD_SIZE)
    outputs = attn_out.reshape(tok_rows, heads_local, HEAD_SIZE)
    row_delta = jnp.sum(out_grads.astype(jnp.float32) * outputs.astype(jnp.float32), axis=2)
    delta_heads = row_delta.T[:, :, None]
    lse_heads = log_sums[:, :, None]
    query_heads = query_rows.reshape(tok_rows, heads_local, HEAD_SIZE).transpose(1, 0, 2)
    grad_heads = out_grads.transpose(1, 0, 2)
    query_start = ctx_pos * tok_rows
    z_pos = ctx_pos // Y_HI
    z_count = ctx_count // Y_HI
    y_hi = ctx_pos % Y_HI
    super_rows = Y_HI * tok_rows
    turns = jnp.arange(z_count, dtype=jnp.int32)
    ahead_owner = (z_pos + turns) % z_count
    behind_owner = (z_pos - turns) % z_count
    half_blocks = tok_rows // BLK
    key_block = jnp.concatenate(
        [
            ahead_owner[:, None] * (2 * half_blocks) + jnp.arange(half_blocks)[None, :],
            behind_owner[:, None] * (2 * half_blocks) + half_blocks + jnp.arange(half_blocks)[None, :],
        ],
        axis=1,
    )
    query_block = query_start // BLK + jnp.arange(half_blocks, dtype=jnp.int32)
    qb = query_block[None, :, None]
    kb = key_block[:, None, :]
    allowed = block_mask[qb, kb]
    codes = jnp.where(kb == qb, 2, jnp.where((kb < qb) & (allowed == 1), 1, 0))
    codes = codes.reshape(z_count, -1).astype(jnp.int32)

    def terms(ahead_kv, behind_kv, turn, query_acc):
        turn_index = jnp.reshape(turn, (1,)).astype(jnp.int32)
        return turn_call(
            turn_index,
            codes,
            query_heads,
            grad_heads,
            ahead_kv,
            behind_kv,
            lse_heads,
            delta_heads,
            query_acc,
        )

    key_values = jnp.concatenate([key_matrix, value_matrix], axis=1)
    partner_kv = from_partner(key_values, ctx_count)
    ahead_kv = jnp.where(y_hi == 0, key_values, partner_kv)
    behind_kv = jnp.where(y_hi == 0, partner_kv, key_values)
    next_ahead = along_z(ahead_kv, ctx_count, 1)
    next_behind = along_z(behind_kv, ctx_count, -1)
    zero_query = jnp.zeros((heads_local, tok_rows, HEAD_SIZE), jnp.float32)
    query_acc, ahead_pending, behind_pending = terms(ahead_kv, behind_kv, 0, zero_query)

    def visit_turn(turn, carried):
        ahead_kv, behind_kv, query_acc, ahead_pending, behind_pending = carried
        ahead_received = along_z(ahead_pending, ctx_count, 1)
        behind_received = along_z(behind_pending, ctx_count, -1)
        next_ahead = along_z(ahead_kv, ctx_count, 1)
        next_behind = along_z(behind_kv, ctx_count, -1)
        query_acc, ahead_term, behind_term = terms(ahead_kv, behind_kv, turn, query_acc)
        return (
            next_ahead,
            next_behind,
            query_acc,
            ahead_received + ahead_term,
            behind_received + behind_term,
        )

    ahead_kv, behind_kv, query_acc, ahead_pending, behind_pending = lax.fori_loop(
        1,
        z_count - 1,
        visit_turn,
        (next_ahead, next_behind, query_acc, ahead_pending, behind_pending),
    )
    ahead_received = along_z(ahead_pending, ctx_count, 1)
    behind_received = along_z(behind_pending, ctx_count, -1)
    query_acc, ahead_term, behind_term = terms(ahead_kv, behind_kv, z_count - 1, query_acc)
    ahead_total = along_z(ahead_received + ahead_term, ctx_count, 1)
    behind_total = along_z(behind_received + behind_term, ctx_count, -1)
    own_total = jnp.where(y_hi == 0, ahead_total, behind_total)
    other_total = jnp.where(y_hi == 0, behind_total, ahead_total)
    summed = own_total + from_partner(other_total, ctx_count)
    logit_scale = 1.0 / math.sqrt(HEAD_SIZE)
    query_grad = (query_acc * logit_scale).transpose(1, 0, 2).reshape(tok_rows, col_width)
    query_grad = query_grad.astype(jnp.bfloat16)
    key_gradient = (summed[:, :HEAD_SIZE] * logit_scale).astype(jnp.bfloat16)
    value_gradient = summed[:, HEAD_SIZE:].astype(jnp.bfloat16)
    return (query_grad, key_gradient, value_gradient)


def solution(mesh):
    placed = (
        P(("dp", "ctx"), "tp"),
        P(("dp", "ctx"), "tp"),
        P(("dp", "ctx"), "tp"),
        P(("dp", "ctx"), "tp"),
        P(("dp", "ctx", "tp"), None),
        P("tp", ("dp", "ctx")),
        P("dp", None),
    )
    return jax.shard_map(
        local,
        mesh=mesh,
        in_specs=placed,
        out_specs=(P(("dp", "ctx"), "tp"), P(("dp", "ctx"), "tp"), P(("dp", "ctx"), "tp")),
        check_vma=False,
    )
```

```python
import math

import jax
import jax.numpy as jnp
from jax import lax
from jax.experimental import pallas as pl
from jax.experimental.pallas import tpu as pltpu
from jax.sharding import PartitionSpec as P

BLK = 128
HEAD_SIZE = 128
Y_HI = 2


def along_z(value, ctx_count, shift):
    z_count = ctx_count // Y_HI
    pairs = [
        (Y_HI * ((z + shift) % z_count) + h, Y_HI * z + h)
        for z in range(z_count)
        for h in range(Y_HI)
    ]
    return lax.ppermute(value, "ctx", pairs)


def from_partner(value, ctx_count):
    pairs = [(c, c ^ 1) for c in range(ctx_count)]
    return lax.ppermute(value, "ctx", pairs)


def turn_kernel(turn_ref, code_ref, q_ref, do_ref, ahead_kv_ref, behind_kv_ref, lse_ref, delta_ref,
                dq_in_ref, ahead_in_ref, behind_in_ref, dq_ref, ahead_ref, behind_ref):
    heads, tok_rows, _ = q_ref.shape
    half = ahead_kv_ref.shape[0]
    key_count = 2 * half
    row_blocks = tok_rows // BLK
    key_blocks = key_count // BLK
    scale = 1.0 / math.sqrt(HEAD_SIZE)
    turn = turn_ref[0]
    key_row = lax.broadcasted_iota(jnp.int32, (key_count, tok_rows), 0)
    query_col = lax.broadcasted_iota(jnp.int32, (key_count, tok_rows), 1)
    key_block = key_row // BLK
    query_block = query_col // BLK
    code = jnp.zeros((key_count, tok_rows), jnp.int32)
    for r in range(row_blocks):
        for c in range(key_blocks):
            code = jnp.where((query_block == r) & (key_block == c), code_ref[turn, r * key_blocks + c], code)
    below = (key_row - key_block * BLK) <= (query_col - query_block * BLK)
    live = (code == 1) | ((code == 2) & below)
    keys = jnp.concatenate([ahead_kv_ref[:, :HEAD_SIZE], behind_kv_ref[:, :HEAD_SIZE]], axis=0)
    values = jnp.concatenate([ahead_kv_ref[:, HEAD_SIZE:], behind_kv_ref[:, HEAD_SIZE:]], axis=0)
    dk = jnp.zeros((key_count, HEAD_SIZE), jnp.float32)
    dv = jnp.zeros((key_count, HEAD_SIZE), jnp.float32)
    for h in range(heads):
        q = q_ref[h]
        do = do_ref[h]
        st = lax.dot_general(keys, q, (((1,), (1,)), ((), ())), preferred_element_type=jnp.float32)
        pt = jnp.where(live, jnp.exp(st * scale - lse_ref[h]), 0.0)
        dpt = lax.dot_general(values, do, (((1,), (1,)), ((), ())), preferred_element_type=jnp.float32)
        dst = (pt * (dpt - delta_ref[h])).astype(jnp.bfloat16).astype(keys.dtype)
        dq_ref[h] = dq_in_ref[h] + lax.dot_general(
            dst, keys, (((0,), (0,)), ((), ())), preferred_element_type=jnp.float32
        )
        dk = dk + jnp.dot(dst, q, preferred_element_type=jnp.float32)
        dv = dv + jnp.dot(pt.astype(jnp.bfloat16).astype(do.dtype), do, preferred_element_type=jnp.float32)
    ahead_ref[:, :HEAD_SIZE] = ahead_in_ref[:, :HEAD_SIZE] + dk[:half]
    ahead_ref[:, HEAD_SIZE:] = ahead_in_ref[:, HEAD_SIZE:] + dv[:half]
    behind_ref[:, :HEAD_SIZE] = behind_in_ref[:, :HEAD_SIZE] + dk[half:]
    behind_ref[:, HEAD_SIZE:] = behind_in_ref[:, HEAD_SIZE:] + dv[half:]


def turn_call(turn, codes, q, do, ahead_kv, behind_kv, lse, delta, dq_acc, ahead_in, behind_in):
    vmem = pl.BlockSpec(memory_space=pltpu.MemorySpace.VMEM)
    smem = pl.BlockSpec(memory_space=pltpu.MemorySpace.SMEM)
    return pl.pallas_call(
        turn_kernel,
        out_shape=(
            jax.ShapeDtypeStruct(dq_acc.shape, jnp.float32),
            jax.ShapeDtypeStruct(ahead_in.shape, jnp.float32),
            jax.ShapeDtypeStruct(behind_in.shape, jnp.float32),
        ),
        in_specs=[smem, smem] + [vmem] * 9,
        out_specs=(vmem, vmem, vmem),
        input_output_aliases={8: 0, 9: 1, 10: 2},
    )(turn, codes, q, do, ahead_kv, behind_kv, lse, delta, dq_acc, ahead_in, behind_in)


def local(query_rows, key_matrix, value_matrix, attn_out, out_grad, log_sums, block_mask):
    tok_rows = query_rows.shape[0]
    col_width = query_rows.shape[1]
    heads_local = col_width // HEAD_SIZE
    ctx_pos = lax.axis_index("ctx")
    ctx_count = lax.axis_size("ctx")
    tp_count = lax.axis_size("tp")
    grad_rows = out_grad.shape[0]
    pieces = out_grad.reshape(grad_rows, tp_count, col_width)
    own_grad = lax.all_to_all(pieces, "tp", split_axis=1, concat_axis=0, tiled=True)
    out_grads = own_grad.reshape(tok_rows, heads_local, HEAD_SIZE)
    outputs = attn_out.reshape(tok_rows, heads_local, HEAD_SIZE)
    row_delta = jnp.sum(out_grads.astype(jnp.float32) * outputs.astype(jnp.float32), axis=2)
    delta_heads = row_delta.T[:, None, :]
    lse_heads = log_sums[:, None, :]
    query_heads = query_rows.reshape(tok_rows, heads_local, HEAD_SIZE).transpose(1, 0, 2)
    grad_heads = out_grads.transpose(1, 0, 2)
    query_start = ctx_pos * tok_rows
    z_pos = ctx_pos // Y_HI
    z_count = ctx_count // Y_HI
    y_hi = ctx_pos % Y_HI
    super_rows = Y_HI * tok_rows
    turns = jnp.arange(z_count, dtype=jnp.int32)
    ahead_owner = (z_pos + turns) % z_count
    behind_owner = (z_pos - turns) % z_count
    half_blocks = tok_rows // BLK
    key_block = jnp.concatenate(
        [
            ahead_owner[:, None] * (2 * half_blocks) + jnp.arange(half_blocks)[None, :],
            behind_owner[:, None] * (2 * half_blocks) + half_blocks + jnp.arange(half_blocks)[None, :],
        ],
        axis=1,
    )
    query_block = query_start // BLK + jnp.arange(half_blocks, dtype=jnp.int32)
    qb = query_block[None, :, None]
    kb = key_block[:, None, :]
    allowed = block_mask[qb, kb]
    codes = jnp.where(kb == qb, 2, jnp.where((kb < qb) & (allowed == 1), 1, 0))
    codes = codes.reshape(z_count, -1).astype(jnp.int32)

    def terms(ahead_kv, behind_kv, turn, query_acc, ahead_in, behind_in):
        turn_index = jnp.reshape(turn, (1,)).astype(jnp.int32)
        return turn_call(
            turn_index,
            codes,
            query_heads,
            grad_heads,
            ahead_kv,
            behind_kv,
            lse_heads,
            delta_heads,
            query_acc,
            ahead_in,
            behind_in,
        )

    key_values = jnp.concatenate([key_matrix, value_matrix], axis=1)
    partner_kv = from_partner(key_values, ctx_count)
    ahead_kv = jnp.where(y_hi == 0, key_values, partner_kv)
    behind_kv = jnp.where(y_hi == 0, partner_kv, key_values)
    next_ahead = along_z(ahead_kv, ctx_count, 1)
    next_behind = along_z(behind_kv, ctx_count, -1)
    zero_query = jnp.zeros((heads_local, tok_rows, HEAD_SIZE), jnp.float32)
    zero_total = jnp.zeros((tok_rows, 2 * HEAD_SIZE), jnp.float32)
    query_acc, ahead_pending, behind_pending = terms(
        ahead_kv, behind_kv, 0, zero_query, zero_total, zero_total
    )

    def visit_turn(turn, carried):
        ahead_kv, behind_kv, query_acc, ahead_pending, behind_pending = carried
        ahead_received = along_z(ahead_pending, ctx_count, 1)
        behind_received = along_z(behind_pending, ctx_count, -1)
        next_ahead = along_z(ahead_kv, ctx_count, 1)
        next_behind = along_z(behind_kv, ctx_count, -1)
        query_acc, ahead_pending, behind_pending = terms(
            ahead_kv, behind_kv, turn, query_acc, ahead_received, behind_received
        )
        return (next_ahead, next_behind, query_acc, ahead_pending, behind_pending)

    ahead_kv, behind_kv, query_acc, ahead_pending, behind_pending = lax.fori_loop(
        1,
        z_count - 1,
        visit_turn,
        (next_ahead, next_behind, query_acc, ahead_pending, behind_pending),
    )
    ahead_received = along_z(ahead_pending, ctx_count, 1)
    behind_received = along_z(behind_pending, ctx_count, -1)
    query_acc, ahead_pending, behind_pending = terms(
        ahead_kv, behind_kv, z_count - 1, query_acc, ahead_received, behind_received
    )
    ahead_total = along_z(ahead_pending, ctx_count, 1)
    behind_total = along_z(behind_pending, ctx_count, -1)
    own_total = jnp.where(y_hi == 0, ahead_total, behind_total)
    other_total = jnp.where(y_hi == 0, behind_total, ahead_total)
    summed = own_total + from_partner(other_total, ctx_count)
    logit_scale = 1.0 / math.sqrt(HEAD_SIZE)
    query_grad = (query_acc * logit_scale).transpose(1, 0, 2).reshape(tok_rows, col_width)
    query_grad = query_grad.astype(jnp.bfloat16)
    key_gradient = (summed[:, :HEAD_SIZE] * logit_scale).astype(jnp.bfloat16)
    value_gradient = summed[:, HEAD_SIZE:].astype(jnp.bfloat16)
    return (query_grad, key_gradient, value_gradient)


def solution(mesh):
    placed = (
        P(("dp", "ctx"), "tp"),
        P(("dp", "ctx"), "tp"),
        P(("dp", "ctx"), "tp"),
        P(("dp", "ctx"), "tp"),
        P(("dp", "ctx", "tp"), None),
        P("tp", ("dp", "ctx")),
        P("dp", None),
    )
    return jax.shard_map(
        local,
        mesh=mesh,
        in_specs=placed,
        out_specs=(P(("dp", "ctx"), "tp"), P(("dp", "ctx"), "tp"), P(("dp", "ctx"), "tp")),
        check_vma=False,
    )
```

```python
import math

import jax
import jax.numpy as jnp
from jax import lax
from jax.sharding import PartitionSpec as P

BLK = 128
HEAD_SIZE = 128
Y_HI = 2


def along_z(value, ctx_count, shift):
    z_count = ctx_count // Y_HI
    pairs = [
        (Y_HI * ((z + shift) % z_count) + h, Y_HI * z + h)
        for z in range(z_count)
        for h in range(Y_HI)
    ]
    return lax.ppermute(value, "ctx", pairs)


def to_owner(value, ctx_count, ring_half):
    z_count = ctx_count // Y_HI
    pairs = []
    for z in range(z_count):
        for h in range(Y_HI):
            first = (h == 0) == (ring_half == 0)
            target = Y_HI * ((z - 1) % z_count) if first else Y_HI * ((z + 1) % z_count) + 1
            pairs.append((Y_HI * z + h, target))
    return lax.ppermute(value, "ctx", pairs)


def from_partner(value, ctx_count):
    pairs = [(c, c ^ 1) for c in range(ctx_count)]
    return lax.ppermute(value, "ctx", pairs)


def live_region(block_mask, query_start, tok_rows, key_pos):
    query_rows = lax.dynamic_slice_in_dim(block_mask, query_start // BLK, tok_rows // BLK, 0)
    block_table = jnp.take(query_rows, key_pos[::BLK] // BLK, axis=1)
    block_table = jnp.repeat(jnp.repeat(block_table, BLK, axis=0), BLK, axis=1)
    query_pos = query_start + jnp.arange(tok_rows, dtype=jnp.int32)
    query_block = (query_pos // BLK)[:, None]
    key_block = (key_pos // BLK)[None, :]
    earlier = (key_block < query_block) & (block_table == 1)
    diagonal = (key_block == query_block) & (key_pos[None, :] <= query_pos[:, None])
    return earlier | diagonal


def contract(queries, out_grads, row_delta, log_sums, keys_part, values_part, live_mask):
    logit_scale = 1.0 / math.sqrt(HEAD_SIZE)
    scores = (
        jnp.einsum("igd,jd->gij", queries, keys_part, preferred_element_type=jnp.float32)
        * logit_scale
    )
    probabilities = jnp.where(live_mask[None], jnp.exp(scores - log_sums[:, :, None]), 0.0)
    prob_grad = jnp.einsum(
        "igd,jd->gij", out_grads, values_part, preferred_element_type=jnp.float32
    )
    dscore = (probabilities * (prob_grad - row_delta[:, :, None])).astype(jnp.bfloat16)
    query_term = jnp.einsum("gij,jd->igd", dscore, keys_part, preferred_element_type=jnp.float32)
    key_term = jnp.einsum("gij,igd->jd", dscore, queries, preferred_element_type=jnp.float32)
    value_term = jnp.einsum(
        "gij,igd->jd",
        probabilities.astype(jnp.bfloat16),
        out_grads,
        preferred_element_type=jnp.float32,
    )
    return (query_term, key_term, value_term)


def local(query_rows, key_matrix, value_matrix, attn_out, out_grad, log_sums, block_mask):
    tok_rows = query_rows.shape[0]
    col_width = query_rows.shape[1]
    heads_local = col_width // HEAD_SIZE
    ctx_pos = lax.axis_index("ctx")
    ctx_count = lax.axis_size("ctx")
    tp_count = lax.axis_size("tp")
    grad_rows = out_grad.shape[0]
    pieces = out_grad.reshape(grad_rows, tp_count, col_width)
    own_grad = lax.all_to_all(pieces, "tp", split_axis=1, concat_axis=0, tiled=True)
    queries = query_rows.reshape(tok_rows, heads_local, HEAD_SIZE)
    out_grads = own_grad.reshape(tok_rows, heads_local, HEAD_SIZE)
    outputs = attn_out.reshape(tok_rows, heads_local, HEAD_SIZE)
    row_delta = jnp.sum(out_grads.astype(jnp.float32) * outputs.astype(jnp.float32), axis=2).T
    query_start = ctx_pos * tok_rows
    z_pos = ctx_pos // Y_HI
    z_count = ctx_count // Y_HI
    y_hi = ctx_pos % Y_HI
    super_rows = Y_HI * tok_rows
    offsets = jnp.arange(tok_rows, dtype=jnp.int32)

    def terms(ahead_kv, behind_kv, turn):
        ahead_owner = (z_pos + turn) % z_count
        behind_owner = (z_pos - turn) % z_count
        key_pos = jnp.concatenate(
            [ahead_owner * super_rows + offsets, behind_owner * super_rows + tok_rows + offsets]
        )
        live_mask = live_region(block_mask, query_start, tok_rows, key_pos)
        key_values = jnp.concatenate([ahead_kv, behind_kv], axis=0)
        query_term, key_term, value_term = contract(
            queries,
            out_grads,
            row_delta,
            log_sums,
            key_values[:, :HEAD_SIZE],
            key_values[:, HEAD_SIZE:],
            live_mask,
        )
        kv_term = jnp.concatenate([key_term, value_term], axis=1)
        return query_term, kv_term[:tok_rows], kv_term[tok_rows:]

    key_values = jnp.concatenate([key_matrix, value_matrix], axis=1)
    partner_kv = from_partner(key_values, ctx_count)
    ahead_kv = jnp.where(y_hi == 0, key_values, partner_kv)
    behind_kv = jnp.where(y_hi == 0, partner_kv, key_values)
    next_ahead = along_z(ahead_kv, ctx_count, 1)
    next_behind = along_z(behind_kv, ctx_count, -1)
    query_acc, ahead_pending, behind_pending = terms(ahead_kv, behind_kv, 0)

    def visit_turn(turn, carried):
        ahead_kv, behind_kv, query_acc, ahead_pending, behind_pending = carried
        ahead_received = along_z(ahead_pending, ctx_count, 1)
        behind_received = along_z(behind_pending, ctx_count, -1)
        next_ahead = along_z(ahead_kv, ctx_count, 1)
        next_behind = along_z(behind_kv, ctx_count, -1)
        query_term, ahead_term, behind_term = terms(ahead_kv, behind_kv, turn)
        return (
            next_ahead,
            next_behind,
            query_acc + query_term,
            ahead_received + ahead_term,
            behind_received + behind_term,
        )

    ahead_kv, behind_kv, query_acc, ahead_pending, behind_pending = lax.fori_loop(
        1,
        z_count - 1,
        visit_turn,
        (next_ahead, next_behind, query_acc, ahead_pending, behind_pending),
    )
    ahead_received = along_z(ahead_pending, ctx_count, 1)
    behind_received = along_z(behind_pending, ctx_count, -1)
    query_term, ahead_term, behind_term = terms(ahead_kv, behind_kv, z_count - 1)
    query_acc = query_acc + query_term
    ahead_final = ahead_received + ahead_term
    behind_final = behind_received + behind_term
    same_ring = jnp.where(y_hi == 0, ahead_final, behind_final)
    other_ring = jnp.where(y_hi == 0, behind_final, ahead_final)
    summed = to_owner(same_ring, ctx_count, 0) + to_owner(other_ring, ctx_count, 1)
    logit_scale = 1.0 / math.sqrt(HEAD_SIZE)
    query_grad = (query_acc * logit_scale).reshape(tok_rows, col_width).astype(jnp.bfloat16)
    key_gradient = (summed[:, :HEAD_SIZE] * logit_scale).astype(jnp.bfloat16)
    value_gradient = summed[:, HEAD_SIZE:].astype(jnp.bfloat16)
    return (query_grad, key_gradient, value_gradient)


def solution(mesh):
    placed = (
        P(("dp", "ctx"), "tp"),
        P(("dp", "ctx"), "tp"),
        P(("dp", "ctx"), "tp"),
        P(("dp", "ctx"), "tp"),
        P(("dp", "ctx", "tp"), None),
        P("tp", ("dp", "ctx")),
        P("dp", None),
    )
    return jax.shard_map(
        local,
        mesh=mesh,
        in_specs=placed,
        out_specs=(P(("dp", "ctx"), "tp"), P(("dp", "ctx"), "tp"), P(("dp", "ctx"), "tp")),
        check_vma=False,
    )
```

```python
import math

import jax
import jax.numpy as jnp
from jax import lax
from jax.sharding import PartitionSpec as P

BLK = 128
HEAD_SIZE = 128
Y_HI = 2


def along_z(value, ctx_count, shift):
    z_count = ctx_count // Y_HI
    pairs = [
        (Y_HI * ((z + shift) % z_count) + h, Y_HI * z + h)
        for z in range(z_count)
        for h in range(Y_HI)
    ]
    return lax.ppermute(value, "ctx", pairs)


def to_owner(value, ctx_count, ring_half):
    z_count = ctx_count // Y_HI
    pairs = []
    for z in range(z_count):
        for h in range(Y_HI):
            first = (h == 0) == (ring_half == 0)
            target = Y_HI * ((z - 1) % z_count) if first else Y_HI * ((z + 1) % z_count) + 1
            pairs.append((Y_HI * z + h, target))
    return lax.ppermute(value, "ctx", pairs)


def from_partner(value, ctx_count):
    pairs = [(c, c ^ 1) for c in range(ctx_count)]
    return lax.ppermute(value, "ctx", pairs)


def live_region(block_mask, query_start, tok_rows, key_pos):
    query_rows = lax.dynamic_slice_in_dim(block_mask, query_start // BLK, tok_rows // BLK, 0)
    block_table = jnp.take(query_rows, key_pos[::BLK] // BLK, axis=1)
    block_table = jnp.repeat(jnp.repeat(block_table, BLK, axis=0), BLK, axis=1)
    query_pos = query_start + jnp.arange(tok_rows, dtype=jnp.int32)
    query_block = (query_pos // BLK)[:, None]
    key_block = (key_pos // BLK)[None, :]
    earlier = (key_block < query_block) & (block_table == 1)
    diagonal = (key_block == query_block) & (key_pos[None, :] <= query_pos[:, None])
    return earlier | diagonal


def contract(queries, out_grads, row_delta, log_sums, keys_part, values_part, live_mask):
    logit_scale = 1.0 / math.sqrt(HEAD_SIZE)
    scores = (
        jnp.einsum("igd,jd->gij", queries, keys_part, preferred_element_type=jnp.float32)
        * logit_scale
    )
    probabilities = jnp.where(live_mask[None], jnp.exp(scores - log_sums[:, :, None]), 0.0)
    prob_grad = jnp.einsum(
        "igd,jd->gij", out_grads, values_part, preferred_element_type=jnp.float32
    )
    dscore = (probabilities * (prob_grad - row_delta[:, :, None])).astype(jnp.bfloat16)
    query_term = jnp.einsum("gij,jd->igd", dscore, keys_part, preferred_element_type=jnp.float32)
    key_term = jnp.einsum("gij,igd->jd", dscore, queries, preferred_element_type=jnp.float32)
    value_term = jnp.einsum(
        "gij,igd->jd",
        probabilities.astype(jnp.bfloat16),
        out_grads,
        preferred_element_type=jnp.float32,
    )
    return (query_term, key_term, value_term)


def local(query_rows, key_matrix, value_matrix, attn_out, out_grad, log_sums, block_mask):
    tok_rows = query_rows.shape[0]
    col_width = query_rows.shape[1]
    heads_local = col_width // HEAD_SIZE
    ctx_pos = lax.axis_index("ctx")
    ctx_count = lax.axis_size("ctx")
    tp_count = lax.axis_size("tp")
    grad_rows = out_grad.shape[0]
    pieces = out_grad.reshape(grad_rows, tp_count, col_width)
    own_grad = lax.all_to_all(pieces, "tp", split_axis=1, concat_axis=0, tiled=True)
    queries = query_rows.reshape(tok_rows, heads_local, HEAD_SIZE)
    out_grads = own_grad.reshape(tok_rows, heads_local, HEAD_SIZE)
    outputs = attn_out.reshape(tok_rows, heads_local, HEAD_SIZE)
    row_delta = jnp.sum(out_grads.astype(jnp.float32) * outputs.astype(jnp.float32), axis=2).T
    query_start = ctx_pos * tok_rows
    z_pos = ctx_pos // Y_HI
    z_count = ctx_count // Y_HI
    y_hi = ctx_pos % Y_HI
    super_rows = Y_HI * tok_rows
    offsets = jnp.arange(tok_rows, dtype=jnp.int32)

    def terms(ahead_kv, behind_kv, turn):
        ahead_owner = (z_pos + turn) % z_count
        behind_owner = (z_pos - turn) % z_count
        key_pos = jnp.concatenate(
            [ahead_owner * super_rows + offsets, behind_owner * super_rows + tok_rows + offsets]
        )
        live_mask = live_region(block_mask, query_start, tok_rows, key_pos)
        key_values = jnp.concatenate([ahead_kv, behind_kv], axis=0)
        query_term, key_term, value_term = contract(
            queries,
            out_grads,
            row_delta,
            log_sums,
            key_values[:, :HEAD_SIZE],
            key_values[:, HEAD_SIZE:],
            live_mask,
        )
        kv_term = jnp.concatenate([key_term, value_term], axis=1)
        return query_term, kv_term[:tok_rows], kv_term[tok_rows:]

    key_values = jnp.concatenate([key_matrix, value_matrix], axis=1)
    partner_kv = from_partner(key_values, ctx_count)
    ahead_kv = jnp.where(y_hi == 0, key_values, partner_kv)
    behind_kv = jnp.where(y_hi == 0, partner_kv, key_values)
    next_ahead = along_z(ahead_kv, ctx_count, 1)
    next_behind = along_z(behind_kv, ctx_count, -1)
    query_acc, ahead_pending, behind_pending = terms(ahead_kv, behind_kv, 0)

    kv_width = key_values.shape[1]

    def bundled(kv, pending, shift):
        both = jnp.concatenate([kv.astype(jnp.float32), pending], axis=1)
        moved = along_z(both, ctx_count, shift)
        return moved[:, :kv_width].astype(kv.dtype), moved[:, kv_width:]

    def visit_turn(turn, carried):
        ahead_kv, behind_kv, query_acc, ahead_pending, behind_pending = carried
        next_ahead, ahead_received = bundled(ahead_kv, ahead_pending, 1)
        next_behind, behind_received = bundled(behind_kv, behind_pending, -1)
        query_term, ahead_term, behind_term = terms(ahead_kv, behind_kv, turn)
        return (
            next_ahead,
            next_behind,
            query_acc + query_term,
            ahead_received + ahead_term,
            behind_received + behind_term,
        )

    ahead_kv, behind_kv, query_acc, ahead_pending, behind_pending = lax.fori_loop(
        1,
        z_count - 1,
        visit_turn,
        (next_ahead, next_behind, query_acc, ahead_pending, behind_pending),
    )
    ahead_received = along_z(ahead_pending, ctx_count, 1)
    behind_received = along_z(behind_pending, ctx_count, -1)
    query_term, ahead_term, behind_term = terms(ahead_kv, behind_kv, z_count - 1)
    query_acc = query_acc + query_term
    ahead_final = ahead_received + ahead_term
    behind_final = behind_received + behind_term
    same_ring = jnp.where(y_hi == 0, ahead_final, behind_final)
    other_ring = jnp.where(y_hi == 0, behind_final, ahead_final)
    summed = to_owner(same_ring, ctx_count, 0) + to_owner(other_ring, ctx_count, 1)
    logit_scale = 1.0 / math.sqrt(HEAD_SIZE)
    query_grad = (query_acc * logit_scale).reshape(tok_rows, col_width).astype(jnp.bfloat16)
    key_gradient = (summed[:, :HEAD_SIZE] * logit_scale).astype(jnp.bfloat16)
    value_gradient = summed[:, HEAD_SIZE:].astype(jnp.bfloat16)
    return (query_grad, key_gradient, value_gradient)


def solution(mesh):
    placed = (
        P(("dp", "ctx"), "tp"),
        P(("dp", "ctx"), "tp"),
        P(("dp", "ctx"), "tp"),
        P(("dp", "ctx"), "tp"),
        P(("dp", "ctx", "tp"), None),
        P("tp", ("dp", "ctx")),
        P("dp", None),
    )
    return jax.shard_map(
        local,
        mesh=mesh,
        in_specs=placed,
        out_specs=(P(("dp", "ctx"), "tp"), P(("dp", "ctx"), "tp"), P(("dp", "ctx"), "tp")),
        check_vma=False,
    )
```

```python
import math

import jax
import jax.numpy as jnp
from jax import lax
from jax.sharding import PartitionSpec as P

BLK = 128
HEAD_SIZE = 128
Y_HI = 2


def along_z(value, ctx_count, shift):
    z_count = ctx_count // Y_HI
    pairs = [
        (Y_HI * ((z + shift) % z_count) + h, Y_HI * z + h)
        for z in range(z_count)
        for h in range(Y_HI)
    ]
    return lax.ppermute(value, "ctx", pairs)


def to_owner(value, ctx_count, ring_half):
    z_count = ctx_count // Y_HI
    pairs = []
    for z in range(z_count):
        for h in range(Y_HI):
            first = (h == 0) == (ring_half == 0)
            target = Y_HI * ((z - 1) % z_count) if first else Y_HI * ((z + 1) % z_count) + 1
            pairs.append((Y_HI * z + h, target))
    return lax.ppermute(value, "ctx", pairs)


def from_partner(value, ctx_count):
    pairs = [(c, c ^ 1) for c in range(ctx_count)]
    return lax.ppermute(value, "ctx", pairs)


def live_region(block_mask, query_start, tok_rows, key_pos):
    query_rows = lax.dynamic_slice_in_dim(block_mask, query_start // BLK, tok_rows // BLK, 0)
    block_table = jnp.take(query_rows, key_pos[::BLK] // BLK, axis=1)
    block_table = jnp.repeat(jnp.repeat(block_table, BLK, axis=0), BLK, axis=1)
    query_pos = query_start + jnp.arange(tok_rows, dtype=jnp.int32)
    query_block = (query_pos // BLK)[:, None]
    key_block = (key_pos // BLK)[None, :]
    earlier = (key_block < query_block) & (block_table == 1)
    diagonal = (key_block == query_block) & (key_pos[None, :] <= query_pos[:, None])
    return earlier | diagonal


def contract(queries, out_grads, row_delta, log_sums, keys_part, values_part, live_mask):
    logit_scale = 1.0 / math.sqrt(HEAD_SIZE)
    scores = (
        jnp.einsum("igd,jd->gij", queries, keys_part, preferred_element_type=jnp.float32)
        * logit_scale
    )
    probabilities = jnp.where(live_mask[None], jnp.exp(scores - log_sums[:, :, None]), 0.0)
    prob_grad = jnp.einsum(
        "igd,jd->gij", out_grads, values_part, preferred_element_type=jnp.float32
    )
    dscore = (probabilities * (prob_grad - row_delta[:, :, None])).astype(jnp.bfloat16)
    query_term = jnp.einsum("gij,jd->igd", dscore, keys_part, preferred_element_type=jnp.float32)
    key_term = jnp.einsum("gij,igd->jd", dscore, queries, preferred_element_type=jnp.float32)
    value_term = jnp.einsum(
        "gij,igd->jd",
        probabilities.astype(jnp.bfloat16),
        out_grads,
        preferred_element_type=jnp.float32,
    )
    return (query_term, key_term, value_term)


def local(query_rows, key_matrix, value_matrix, attn_out, out_grad, log_sums, block_mask):
    tok_rows = query_rows.shape[0]
    col_width = query_rows.shape[1]
    heads_local = col_width // HEAD_SIZE
    ctx_pos = lax.axis_index("ctx")
    ctx_count = lax.axis_size("ctx")
    tp_count = lax.axis_size("tp")
    grad_rows = out_grad.shape[0]
    pieces = out_grad.reshape(grad_rows, tp_count, col_width)
    own_grad = lax.all_to_all(pieces, "tp", split_axis=1, concat_axis=0, tiled=True)
    queries = query_rows.reshape(tok_rows, heads_local, HEAD_SIZE)
    out_grads = own_grad.reshape(tok_rows, heads_local, HEAD_SIZE)
    outputs = attn_out.reshape(tok_rows, heads_local, HEAD_SIZE)
    row_delta = jnp.sum(out_grads.astype(jnp.float32) * outputs.astype(jnp.float32), axis=2).T
    query_start = ctx_pos * tok_rows
    z_pos = ctx_pos // Y_HI
    z_count = ctx_count // Y_HI
    y_hi = ctx_pos % Y_HI
    super_rows = Y_HI * tok_rows
    offsets = jnp.arange(tok_rows, dtype=jnp.int32)

    def key_positions(turn):
        ahead_owner = (z_pos + turn) % z_count
        behind_owner = (z_pos - turn) % z_count
        return jnp.concatenate(
            [ahead_owner * super_rows + offsets, behind_owner * super_rows + tok_rows + offsets]
        )

    all_masks = jax.vmap(
        lambda turn: live_region(block_mask, query_start, tok_rows, key_positions(turn))
    )(jnp.arange(z_count, dtype=jnp.int32))

    def terms(ahead_kv, behind_kv, turn):
        live_mask = lax.dynamic_index_in_dim(all_masks, turn, 0, keepdims=False)
        key_values = jnp.concatenate([ahead_kv, behind_kv], axis=0)
        query_term, key_term, value_term = contract(
            queries,
            out_grads,
            row_delta,
            log_sums,
            key_values[:, :HEAD_SIZE],
            key_values[:, HEAD_SIZE:],
            live_mask,
        )
        kv_term = jnp.concatenate([key_term, value_term], axis=1)
        return query_term, kv_term[:tok_rows], kv_term[tok_rows:]

    key_values = jnp.concatenate([key_matrix, value_matrix], axis=1)
    partner_kv = from_partner(key_values, ctx_count)
    ahead_kv = jnp.where(y_hi == 0, key_values, partner_kv)
    behind_kv = jnp.where(y_hi == 0, partner_kv, key_values)
    next_ahead = along_z(ahead_kv, ctx_count, 1)
    next_behind = along_z(behind_kv, ctx_count, -1)
    query_acc, ahead_pending, behind_pending = terms(ahead_kv, behind_kv, 0)

    def visit_turn(turn, carried):
        ahead_kv, behind_kv, query_acc, ahead_pending, behind_pending = carried
        ahead_received = along_z(ahead_pending, ctx_count, 1)
        behind_received = along_z(behind_pending, ctx_count, -1)
        next_ahead = along_z(ahead_kv, ctx_count, 1)
        next_behind = along_z(behind_kv, ctx_count, -1)
        query_term, ahead_term, behind_term = terms(ahead_kv, behind_kv, turn)
        return (
            next_ahead,
            next_behind,
            query_acc + query_term,
            ahead_received + ahead_term,
            behind_received + behind_term,
        )

    ahead_kv, behind_kv, query_acc, ahead_pending, behind_pending = lax.fori_loop(
        1,
        z_count - 1,
        visit_turn,
        (next_ahead, next_behind, query_acc, ahead_pending, behind_pending),
    )
    ahead_received = along_z(ahead_pending, ctx_count, 1)
    behind_received = along_z(behind_pending, ctx_count, -1)
    query_term, ahead_term, behind_term = terms(ahead_kv, behind_kv, z_count - 1)
    query_acc = query_acc + query_term
    ahead_final = ahead_received + ahead_term
    behind_final = behind_received + behind_term
    same_ring = jnp.where(y_hi == 0, ahead_final, behind_final)
    other_ring = jnp.where(y_hi == 0, behind_final, ahead_final)
    summed = to_owner(same_ring, ctx_count, 0) + to_owner(other_ring, ctx_count, 1)
    logit_scale = 1.0 / math.sqrt(HEAD_SIZE)
    query_grad = (query_acc * logit_scale).reshape(tok_rows, col_width).astype(jnp.bfloat16)
    key_gradient = (summed[:, :HEAD_SIZE] * logit_scale).astype(jnp.bfloat16)
    value_gradient = summed[:, HEAD_SIZE:].astype(jnp.bfloat16)
    return (query_grad, key_gradient, value_gradient)


def solution(mesh):
    placed = (
        P(("dp", "ctx"), "tp"),
        P(("dp", "ctx"), "tp"),
        P(("dp", "ctx"), "tp"),
        P(("dp", "ctx"), "tp"),
        P(("dp", "ctx", "tp"), None),
        P("tp", ("dp", "ctx")),
        P("dp", None),
    )
    return jax.shard_map(
        local,
        mesh=mesh,
        in_specs=placed,
        out_specs=(P(("dp", "ctx"), "tp"), P(("dp", "ctx"), "tp"), P(("dp", "ctx"), "tp")),
        check_vma=False,
    )
```

```python
import math

import jax
import jax.numpy as jnp
from jax import lax
from jax.sharding import PartitionSpec as P

BLK = 128
HEAD_SIZE = 128
Y_HI = 2


def along_z(value, ctx_count, shift):
    z_count = ctx_count // Y_HI
    pairs = [
        (Y_HI * ((z + shift) % z_count) + h, Y_HI * z + h)
        for z in range(z_count)
        for h in range(Y_HI)
    ]
    return lax.ppermute(value, "ctx", pairs)


def to_owner(value, ctx_count, ring_half):
    z_count = ctx_count // Y_HI
    pairs = []
    for z in range(z_count):
        for h in range(Y_HI):
            first = (h == 0) == (ring_half == 0)
            target = Y_HI * ((z - 1) % z_count) if first else Y_HI * ((z + 1) % z_count) + 1
            pairs.append((Y_HI * z + h, target))
    return lax.ppermute(value, "ctx", pairs)


def from_partner(value, ctx_count):
    pairs = [(c, c ^ 1) for c in range(ctx_count)]
    return lax.ppermute(value, "ctx", pairs)


def live_region(block_mask, query_start, tok_rows, key_pos):
    query_rows = lax.dynamic_slice_in_dim(block_mask, query_start // BLK, tok_rows // BLK, 0)
    block_table = jnp.take(query_rows, key_pos[::BLK] // BLK, axis=1)
    block_table = jnp.repeat(jnp.repeat(block_table, BLK, axis=0), BLK, axis=1)
    query_pos = query_start + jnp.arange(tok_rows, dtype=jnp.int32)
    query_block = (query_pos // BLK)[:, None]
    key_block = (key_pos // BLK)[None, :]
    earlier = (key_block < query_block) & (block_table == 1)
    diagonal = (key_block == query_block) & (key_pos[None, :] <= query_pos[:, None])
    return earlier | diagonal


def contract(queries, out_grads, row_delta, log_sums, keys_part, values_part, live_mask):
    logit_scale = 1.0 / math.sqrt(HEAD_SIZE)
    scores = (
        jnp.einsum("igd,jd->gij", queries, keys_part, preferred_element_type=jnp.float32)
        * logit_scale
    )
    probabilities = jnp.where(live_mask[None], jnp.exp(scores - log_sums[:, :, None]), 0.0)
    prob_grad = jnp.einsum(
        "igd,jd->gij", out_grads, values_part, preferred_element_type=jnp.float32
    )
    dscore = (probabilities * (prob_grad - row_delta[:, :, None])).astype(jnp.bfloat16)
    query_term = jnp.einsum("gij,jd->igd", dscore, keys_part, preferred_element_type=jnp.float32)
    key_term = jnp.einsum("gij,igd->jd", dscore, queries, preferred_element_type=jnp.float32)
    value_term = jnp.einsum(
        "gij,igd->jd",
        probabilities.astype(jnp.bfloat16),
        out_grads,
        preferred_element_type=jnp.float32,
    )
    return (query_term, key_term, value_term)


def local(query_rows, key_matrix, value_matrix, attn_out, out_grad, log_sums, block_mask):
    tok_rows = query_rows.shape[0]
    col_width = query_rows.shape[1]
    heads_local = col_width // HEAD_SIZE
    ctx_pos = lax.axis_index("ctx")
    ctx_count = lax.axis_size("ctx")
    tp_count = lax.axis_size("tp")
    grad_rows = out_grad.shape[0]
    pieces = out_grad.reshape(grad_rows, tp_count, col_width)
    own_grad = lax.all_to_all(pieces, "tp", split_axis=1, concat_axis=0, tiled=True)
    queries = query_rows.reshape(tok_rows, heads_local, HEAD_SIZE)
    out_grads = own_grad.reshape(tok_rows, heads_local, HEAD_SIZE)
    outputs = attn_out.reshape(tok_rows, heads_local, HEAD_SIZE)
    row_delta = jnp.sum(out_grads.astype(jnp.float32) * outputs.astype(jnp.float32), axis=2).T
    query_start = ctx_pos * tok_rows
    z_pos = ctx_pos // Y_HI
    z_count = ctx_count // Y_HI
    y_hi = ctx_pos % Y_HI
    super_rows = Y_HI * tok_rows
    offsets = jnp.arange(tok_rows, dtype=jnp.int32)

    def terms(ahead_kv, behind_kv, turn):
        ahead_owner = (z_pos + turn) % z_count
        behind_owner = (z_pos - turn) % z_count
        key_pos = jnp.concatenate(
            [ahead_owner * super_rows + offsets, behind_owner * super_rows + tok_rows + offsets]
        )
        live_mask = live_region(block_mask, query_start, tok_rows, key_pos)
        key_values = jnp.concatenate([ahead_kv, behind_kv], axis=0)
        query_term, key_term, value_term = contract(
            queries,
            out_grads,
            row_delta,
            log_sums,
            key_values[:, :HEAD_SIZE],
            key_values[:, HEAD_SIZE:],
            live_mask,
        )
        kv_term = jnp.concatenate([key_term, value_term], axis=1)
        return query_term, kv_term[:tok_rows], kv_term[tok_rows:]

    key_values = jnp.concatenate([key_matrix, value_matrix], axis=1)
    partner_kv = from_partner(key_values, ctx_count)
    ahead_kv = jnp.where(y_hi == 0, key_values, partner_kv)
    behind_kv = jnp.where(y_hi == 0, partner_kv, key_values)
    next_ahead = along_z(ahead_kv, ctx_count, 1)
    next_behind = along_z(behind_kv, ctx_count, -1)
    query_acc, ahead_pending, behind_pending = terms(ahead_kv, behind_kv, 0)

    def visit_turn(turn, carried):
        ahead_kv, behind_kv, query_acc, ahead_pending, behind_pending = carried
        ahead_received = along_z(ahead_pending, ctx_count, 1)
        behind_received = along_z(behind_pending, ctx_count, -1)
        next_ahead = along_z(ahead_kv, ctx_count, 1)
        next_behind = along_z(behind_kv, ctx_count, -1)
        query_term, ahead_term, behind_term = terms(ahead_kv, behind_kv, turn)
        return (
            next_ahead,
            next_behind,
            query_acc + query_term,
            ahead_received + ahead_term,
            behind_received + behind_term,
        )

    def visit_two(pair_index, carried):
        carried = visit_turn(2 * pair_index + 1, carried)
        return visit_turn(2 * pair_index + 2, carried)

    ahead_kv, behind_kv, query_acc, ahead_pending, behind_pending = lax.fori_loop(
        0,
        (z_count - 2) // 2,
        visit_two,
        (next_ahead, next_behind, query_acc, ahead_pending, behind_pending),
    )
    ahead_received = along_z(ahead_pending, ctx_count, 1)
    behind_received = along_z(behind_pending, ctx_count, -1)
    query_term, ahead_term, behind_term = terms(ahead_kv, behind_kv, z_count - 1)
    query_acc = query_acc + query_term
    ahead_final = ahead_received + ahead_term
    behind_final = behind_received + behind_term
    same_ring = jnp.where(y_hi == 0, ahead_final, behind_final)
    other_ring = jnp.where(y_hi == 0, behind_final, ahead_final)
    summed = to_owner(same_ring, ctx_count, 0) + to_owner(other_ring, ctx_count, 1)
    logit_scale = 1.0 / math.sqrt(HEAD_SIZE)
    query_grad = (query_acc * logit_scale).reshape(tok_rows, col_width).astype(jnp.bfloat16)
    key_gradient = (summed[:, :HEAD_SIZE] * logit_scale).astype(jnp.bfloat16)
    value_gradient = summed[:, HEAD_SIZE:].astype(jnp.bfloat16)
    return (query_grad, key_gradient, value_gradient)


def solution(mesh):
    placed = (
        P(("dp", "ctx"), "tp"),
        P(("dp", "ctx"), "tp"),
        P(("dp", "ctx"), "tp"),
        P(("dp", "ctx"), "tp"),
        P(("dp", "ctx", "tp"), None),
        P("tp", ("dp", "ctx")),
        P("dp", None),
    )
    return jax.shard_map(
        local,
        mesh=mesh,
        in_specs=placed,
        out_specs=(P(("dp", "ctx"), "tp"), P(("dp", "ctx"), "tp"), P(("dp", "ctx"), "tp")),
        check_vma=False,
    )
```

```python
import math

import jax
import jax.numpy as jnp
from jax import lax
from jax.sharding import PartitionSpec as P

BLK = 128
HEAD_SIZE = 128
Y_HI = 2


def along_z(value, ctx_count, shift):
    z_count = ctx_count // Y_HI
    pairs = [
        (Y_HI * ((z + shift) % z_count) + h, Y_HI * z + h)
        for z in range(z_count)
        for h in range(Y_HI)
    ]
    return lax.ppermute(value, "ctx", pairs)


def to_owner(value, ctx_count, ring_half):
    z_count = ctx_count // Y_HI
    pairs = []
    for z in range(z_count):
        for h in range(Y_HI):
            first = (h == 0) == (ring_half == 0)
            target = Y_HI * ((z - 1) % z_count) if first else Y_HI * ((z + 1) % z_count) + 1
            pairs.append((Y_HI * z + h, target))
    return lax.ppermute(value, "ctx", pairs)


def from_partner(value, ctx_count):
    pairs = [(c, c ^ 1) for c in range(ctx_count)]
    return lax.ppermute(value, "ctx", pairs)


def live_region(block_mask, query_start, tok_rows, key_pos, key_starts):
    row_count = tok_rows // BLK
    block_table = jnp.concatenate(
        [
            lax.dynamic_slice(block_mask, (query_start // BLK, start // BLK), (row_count, row_count))
            for start in key_starts
        ],
        axis=1,
    )
    block_table = jnp.repeat(jnp.repeat(block_table, BLK, axis=0), BLK, axis=1)
    query_pos = query_start + jnp.arange(tok_rows, dtype=jnp.int32)
    query_block = (query_pos // BLK)[:, None]
    key_block = (key_pos // BLK)[None, :]
    earlier = (key_block < query_block) & (block_table == 1)
    diagonal = (key_block == query_block) & (key_pos[None, :] <= query_pos[:, None])
    return earlier | diagonal


def contract(queries, out_grads, row_delta, log_sums, keys_part, values_part, live_mask):
    logit_scale = 1.0 / math.sqrt(HEAD_SIZE)
    scores = (
        jnp.einsum("igd,jd->gij", queries, keys_part, preferred_element_type=jnp.float32)
        * logit_scale
    )
    probabilities = jnp.where(live_mask[None], jnp.exp(scores - log_sums[:, :, None]), 0.0)
    prob_grad = jnp.einsum(
        "igd,jd->gij", out_grads, values_part, preferred_element_type=jnp.float32
    )
    dscore = (probabilities * (prob_grad - row_delta[:, :, None])).astype(jnp.bfloat16)
    query_term = jnp.einsum("gij,jd->igd", dscore, keys_part, preferred_element_type=jnp.float32)
    key_term = jnp.einsum("gij,igd->jd", dscore, queries, preferred_element_type=jnp.float32)
    value_term = jnp.einsum(
        "gij,igd->jd",
        probabilities.astype(jnp.bfloat16),
        out_grads,
        preferred_element_type=jnp.float32,
    )
    return (query_term, key_term, value_term)


def local(query_rows, key_matrix, value_matrix, attn_out, out_grad, log_sums, block_mask):
    tok_rows = query_rows.shape[0]
    col_width = query_rows.shape[1]
    heads_local = col_width // HEAD_SIZE
    ctx_pos = lax.axis_index("ctx")
    ctx_count = lax.axis_size("ctx")
    tp_count = lax.axis_size("tp")
    grad_rows = out_grad.shape[0]
    pieces = out_grad.reshape(grad_rows, tp_count, col_width)
    own_grad = lax.all_to_all(pieces, "tp", split_axis=1, concat_axis=0, tiled=True)
    queries = query_rows.reshape(tok_rows, heads_local, HEAD_SIZE)
    out_grads = own_grad.reshape(tok_rows, heads_local, HEAD_SIZE)
    outputs = attn_out.reshape(tok_rows, heads_local, HEAD_SIZE)
    row_delta = jnp.sum(out_grads.astype(jnp.float32) * outputs.astype(jnp.float32), axis=2).T
    query_start = ctx_pos * tok_rows
    z_pos = ctx_pos // Y_HI
    z_count = ctx_count // Y_HI
    y_hi = ctx_pos % Y_HI
    super_rows = Y_HI * tok_rows
    offsets = jnp.arange(tok_rows, dtype=jnp.int32)

    def terms(ahead_kv, behind_kv, turn):
        ahead_owner = (z_pos + turn) % z_count
        behind_owner = (z_pos - turn) % z_count
        key_starts = (ahead_owner * super_rows, behind_owner * super_rows + tok_rows)
        key_pos = jnp.concatenate([key_starts[0] + offsets, key_starts[1] + offsets])
        live_mask = live_region(block_mask, query_start, tok_rows, key_pos, key_starts)
        key_values = jnp.concatenate([ahead_kv, behind_kv], axis=0)
        query_term, key_term, value_term = contract(
            queries,
            out_grads,
            row_delta,
            log_sums,
            key_values[:, :HEAD_SIZE],
            key_values[:, HEAD_SIZE:],
            live_mask,
        )
        kv_term = jnp.concatenate([key_term, value_term], axis=1)
        return query_term, kv_term[:tok_rows], kv_term[tok_rows:]

    key_values = jnp.concatenate([key_matrix, value_matrix], axis=1)
    partner_kv = from_partner(key_values, ctx_count)
    ahead_kv = jnp.where(y_hi == 0, key_values, partner_kv)
    behind_kv = jnp.where(y_hi == 0, partner_kv, key_values)
    next_ahead = along_z(ahead_kv, ctx_count, 1)
    next_behind = along_z(behind_kv, ctx_count, -1)
    query_acc, ahead_pending, behind_pending = terms(ahead_kv, behind_kv, 0)

    def visit_turn(turn, carried):
        ahead_kv, behind_kv, query_acc, ahead_pending, behind_pending = carried
        ahead_received = along_z(ahead_pending, ctx_count, 1)
        behind_received = along_z(behind_pending, ctx_count, -1)
        next_ahead = along_z(ahead_kv, ctx_count, 1)
        next_behind = along_z(behind_kv, ctx_count, -1)
        query_term, ahead_term, behind_term = terms(ahead_kv, behind_kv, turn)
        return (
            next_ahead,
            next_behind,
            query_acc + query_term,
            ahead_received + ahead_term,
            behind_received + behind_term,
        )

    ahead_kv, behind_kv, query_acc, ahead_pending, behind_pending = lax.fori_loop(
        1,
        z_count - 1,
        visit_turn,
        (next_ahead, next_behind, query_acc, ahead_pending, behind_pending),
    )
    ahead_received = along_z(ahead_pending, ctx_count, 1)
    behind_received = along_z(behind_pending, ctx_count, -1)
    query_term, ahead_term, behind_term = terms(ahead_kv, behind_kv, z_count - 1)
    query_acc = query_acc + query_term
    ahead_final = ahead_received + ahead_term
    behind_final = behind_received + behind_term
    same_ring = jnp.where(y_hi == 0, ahead_final, behind_final)
    other_ring = jnp.where(y_hi == 0, behind_final, ahead_final)
    summed = to_owner(same_ring, ctx_count, 0) + to_owner(other_ring, ctx_count, 1)
    logit_scale = 1.0 / math.sqrt(HEAD_SIZE)
    query_grad = (query_acc * logit_scale).reshape(tok_rows, col_width).astype(jnp.bfloat16)
    key_gradient = (summed[:, :HEAD_SIZE] * logit_scale).astype(jnp.bfloat16)
    value_gradient = summed[:, HEAD_SIZE:].astype(jnp.bfloat16)
    return (query_grad, key_gradient, value_gradient)


def solution(mesh):
    placed = (
        P(("dp", "ctx"), "tp"),
        P(("dp", "ctx"), "tp"),
        P(("dp", "ctx"), "tp"),
        P(("dp", "ctx"), "tp"),
        P(("dp", "ctx", "tp"), None),
        P("tp", ("dp", "ctx")),
        P("dp", None),
    )
    return jax.shard_map(
        local,
        mesh=mesh,
        in_specs=placed,
        out_specs=(P(("dp", "ctx"), "tp"), P(("dp", "ctx"), "tp"), P(("dp", "ctx"), "tp")),
        check_vma=False,
    )
```

```python
import math

import jax
import jax.numpy as jnp
from jax import lax
from jax.sharding import PartitionSpec as P

BLK = 128
HEAD_SIZE = 128
Y_HI = 2


def along_z(value, ctx_count, shift):
    z_count = ctx_count // Y_HI
    pairs = [
        (Y_HI * ((z + shift) % z_count) + h, Y_HI * z + h)
        for z in range(z_count)
        for h in range(Y_HI)
    ]
    return lax.ppermute(value, "ctx", pairs)


def to_owner(value, ctx_count, ring_half):
    z_count = ctx_count // Y_HI
    pairs = []
    for z in range(z_count):
        for h in range(Y_HI):
            first = (h == 0) == (ring_half == 0)
            target = Y_HI * ((z - 1) % z_count) if first else Y_HI * ((z + 1) % z_count) + 1
            pairs.append((Y_HI * z + h, target))
    return lax.ppermute(value, "ctx", pairs)


def from_partner(value, ctx_count):
    pairs = [(c, c ^ 1) for c in range(ctx_count)]
    return lax.ppermute(value, "ctx", pairs)


def live_region(block_mask, query_start, tok_rows, key_pos, key_starts):
    row_count = tok_rows // BLK
    block_table = jnp.concatenate(
        [
            lax.dynamic_slice(block_mask, (query_start // BLK, start // BLK), (row_count, row_count))
            for start in key_starts
        ],
        axis=1,
    )
    block_table = jnp.repeat(jnp.repeat(block_table, BLK, axis=0), BLK, axis=1)
    query_pos = query_start + jnp.arange(tok_rows, dtype=jnp.int32)
    query_block = (query_pos // BLK)[:, None]
    key_block = (key_pos // BLK)[None, :]
    earlier = (key_block < query_block) & (block_table == 1)
    diagonal = (key_block == query_block) & (key_pos[None, :] <= query_pos[:, None])
    return earlier | diagonal


def contract(queries, out_grads, row_delta, log_sums, keys_part, values_part, live_mask):
    logit_scale = 1.0 / math.sqrt(HEAD_SIZE)
    scores = (
        jnp.einsum("igd,jd->gij", queries, keys_part, preferred_element_type=jnp.float32)
        * logit_scale
    )
    probabilities = jnp.where(live_mask[None], jnp.exp(scores - log_sums[:, :, None]), 0.0)
    prob_grad = jnp.einsum(
        "igd,jd->gij", out_grads, values_part, preferred_element_type=jnp.float32
    )
    dscore = (probabilities * (prob_grad - row_delta[:, :, None])).astype(jnp.bfloat16)
    query_term = jnp.einsum("gij,jd->igd", dscore, keys_part, preferred_element_type=jnp.float32)
    key_term = jnp.einsum("gij,igd->jd", dscore, queries, preferred_element_type=jnp.float32)
    value_term = jnp.einsum(
        "gij,igd->jd",
        probabilities.astype(jnp.bfloat16),
        out_grads,
        preferred_element_type=jnp.float32,
    )
    return (query_term, key_term, value_term)


def local(query_rows, key_matrix, value_matrix, attn_out, out_grad, log_sums, block_mask):
    tok_rows = query_rows.shape[0]
    col_width = query_rows.shape[1]
    heads_local = col_width // HEAD_SIZE
    ctx_pos = lax.axis_index("ctx")
    ctx_count = lax.axis_size("ctx")
    tp_count = lax.axis_size("tp")
    grad_rows = out_grad.shape[0]
    pieces = out_grad.reshape(grad_rows, tp_count, col_width)
    own_grad = lax.all_to_all(pieces, "tp", split_axis=1, concat_axis=0, tiled=True)
    queries = query_rows.reshape(tok_rows, heads_local, HEAD_SIZE)
    out_grads = own_grad.reshape(tok_rows, heads_local, HEAD_SIZE)
    outputs = attn_out.reshape(tok_rows, heads_local, HEAD_SIZE)
    row_delta = jnp.sum(out_grads.astype(jnp.float32) * outputs.astype(jnp.float32), axis=2).T
    query_start = ctx_pos * tok_rows
    z_pos = ctx_pos // Y_HI
    z_count = ctx_count // Y_HI
    y_hi = ctx_pos % Y_HI
    super_rows = Y_HI * tok_rows
    offsets = jnp.arange(tok_rows, dtype=jnp.int32)

    def terms(ahead_kv, behind_kv, turn):
        ahead_owner = (z_pos + turn) % z_count
        behind_owner = (z_pos - turn) % z_count
        key_starts = (ahead_owner * super_rows, behind_owner * super_rows + tok_rows)
        key_pos = jnp.concatenate([key_starts[0] + offsets, key_starts[1] + offsets])
        live_mask = lax.optimization_barrier(
            live_region(block_mask, query_start, tok_rows, key_pos, key_starts)
        )
        key_values = jnp.concatenate([ahead_kv, behind_kv], axis=0)
        query_term, key_term, value_term = contract(
            queries,
            out_grads,
            row_delta,
            log_sums,
            key_values[:, :HEAD_SIZE],
            key_values[:, HEAD_SIZE:],
            live_mask,
        )
        kv_term = jnp.concatenate([key_term, value_term], axis=1)
        return query_term, kv_term[:tok_rows], kv_term[tok_rows:]

    key_values = jnp.concatenate([key_matrix, value_matrix], axis=1)
    partner_kv = from_partner(key_values, ctx_count)
    ahead_kv = jnp.where(y_hi == 0, key_values, partner_kv)
    behind_kv = jnp.where(y_hi == 0, partner_kv, key_values)
    next_ahead = along_z(ahead_kv, ctx_count, 1)
    next_behind = along_z(behind_kv, ctx_count, -1)
    query_acc, ahead_pending, behind_pending = terms(ahead_kv, behind_kv, 0)

    def visit_turn(turn, carried):
        ahead_kv, behind_kv, query_acc, ahead_pending, behind_pending = carried
        ahead_received = along_z(ahead_pending, ctx_count, 1)
        behind_received = along_z(behind_pending, ctx_count, -1)
        next_ahead = along_z(ahead_kv, ctx_count, 1)
        next_behind = along_z(behind_kv, ctx_count, -1)
        query_term, ahead_term, behind_term = terms(ahead_kv, behind_kv, turn)
        return (
            next_ahead,
            next_behind,
            query_acc + query_term,
            ahead_received + ahead_term,
            behind_received + behind_term,
        )

    ahead_kv, behind_kv, query_acc, ahead_pending, behind_pending = lax.fori_loop(
        1,
        z_count - 1,
        visit_turn,
        (next_ahead, next_behind, query_acc, ahead_pending, behind_pending),
    )
    ahead_received = along_z(ahead_pending, ctx_count, 1)
    behind_received = along_z(behind_pending, ctx_count, -1)
    query_term, ahead_term, behind_term = terms(ahead_kv, behind_kv, z_count - 1)
    query_acc = query_acc + query_term
    ahead_final = ahead_received + ahead_term
    behind_final = behind_received + behind_term
    same_ring = jnp.where(y_hi == 0, ahead_final, behind_final)
    other_ring = jnp.where(y_hi == 0, behind_final, ahead_final)
    summed = to_owner(same_ring, ctx_count, 0) + to_owner(other_ring, ctx_count, 1)
    logit_scale = 1.0 / math.sqrt(HEAD_SIZE)
    query_grad = (query_acc * logit_scale).reshape(tok_rows, col_width).astype(jnp.bfloat16)
    key_gradient = (summed[:, :HEAD_SIZE] * logit_scale).astype(jnp.bfloat16)
    value_gradient = summed[:, HEAD_SIZE:].astype(jnp.bfloat16)
    return (query_grad, key_gradient, value_gradient)


def solution(mesh):
    placed = (
        P(("dp", "ctx"), "tp"),
        P(("dp", "ctx"), "tp"),
        P(("dp", "ctx"), "tp"),
        P(("dp", "ctx"), "tp"),
        P(("dp", "ctx", "tp"), None),
        P("tp", ("dp", "ctx")),
        P("dp", None),
    )
    return jax.shard_map(
        local,
        mesh=mesh,
        in_specs=placed,
        out_specs=(P(("dp", "ctx"), "tp"), P(("dp", "ctx"), "tp"), P(("dp", "ctx"), "tp")),
        check_vma=False,
    )
```

```python
import math

import jax
import jax.numpy as jnp
from jax import lax
from jax.sharding import PartitionSpec as P

BLK = 128
HEAD_SIZE = 128
Y_HI = 2


def along_z(value, ctx_count, shift):
    z_count = ctx_count // Y_HI
    pairs = [
        (Y_HI * ((z + shift) % z_count) + h, Y_HI * z + h)
        for z in range(z_count)
        for h in range(Y_HI)
    ]
    return lax.ppermute(value, "ctx", pairs)


def to_owner(value, ctx_count, ring_half):
    z_count = ctx_count // Y_HI
    pairs = []
    for z in range(z_count):
        for h in range(Y_HI):
            first = (h == 0) == (ring_half == 0)
            target = Y_HI * ((z - 1) % z_count) if first else Y_HI * ((z + 1) % z_count) + 1
            pairs.append((Y_HI * z + h, target))
    return lax.ppermute(value, "ctx", pairs)


def from_partner(value, ctx_count):
    pairs = [(c, c ^ 1) for c in range(ctx_count)]
    return lax.ppermute(value, "ctx", pairs)


def live_region(block_mask, query_start, tok_rows, key_pos, key_starts, with_diagonal):
    row_count = tok_rows // BLK
    block_table = jnp.concatenate(
        [
            lax.dynamic_slice(block_mask, (query_start // BLK, start // BLK), (row_count, row_count))
            for start in key_starts
        ],
        axis=1,
    )
    block_table = jnp.repeat(jnp.repeat(block_table, BLK, axis=0), BLK, axis=1)
    query_pos = query_start + jnp.arange(tok_rows, dtype=jnp.int32)
    query_block = (query_pos // BLK)[:, None]
    key_block = (key_pos // BLK)[None, :]
    earlier = (key_block < query_block) & (block_table == 1)
    if not with_diagonal:
        return earlier
    diagonal = (key_block == query_block) & (key_pos[None, :] <= query_pos[:, None])
    return earlier | diagonal


def contract(queries, out_grads, row_delta, log_sums, keys_part, values_part, live_mask):
    logit_scale = 1.0 / math.sqrt(HEAD_SIZE)
    scores = (
        jnp.einsum("igd,jd->gij", queries, keys_part, preferred_element_type=jnp.float32)
        * logit_scale
    )
    probabilities = jnp.where(live_mask[None], jnp.exp(scores - log_sums[:, :, None]), 0.0)
    prob_grad = jnp.einsum(
        "igd,jd->gij", out_grads, values_part, preferred_element_type=jnp.float32
    )
    dscore = (probabilities * (prob_grad - row_delta[:, :, None])).astype(jnp.bfloat16)
    query_term = jnp.einsum("gij,jd->igd", dscore, keys_part, preferred_element_type=jnp.float32)
    key_term = jnp.einsum("gij,igd->jd", dscore, queries, preferred_element_type=jnp.float32)
    value_term = jnp.einsum(
        "gij,igd->jd",
        probabilities.astype(jnp.bfloat16),
        out_grads,
        preferred_element_type=jnp.float32,
    )
    return (query_term, key_term, value_term)


def local(query_rows, key_matrix, value_matrix, attn_out, out_grad, log_sums, block_mask):
    tok_rows = query_rows.shape[0]
    col_width = query_rows.shape[1]
    heads_local = col_width // HEAD_SIZE
    ctx_pos = lax.axis_index("ctx")
    ctx_count = lax.axis_size("ctx")
    tp_count = lax.axis_size("tp")
    grad_rows = out_grad.shape[0]
    pieces = out_grad.reshape(grad_rows, tp_count, col_width)
    own_grad = lax.all_to_all(pieces, "tp", split_axis=1, concat_axis=0, tiled=True)
    queries = query_rows.reshape(tok_rows, heads_local, HEAD_SIZE)
    out_grads = own_grad.reshape(tok_rows, heads_local, HEAD_SIZE)
    outputs = attn_out.reshape(tok_rows, heads_local, HEAD_SIZE)
    row_delta = jnp.sum(out_grads.astype(jnp.float32) * outputs.astype(jnp.float32), axis=2).T
    query_start = ctx_pos * tok_rows
    z_pos = ctx_pos // Y_HI
    z_count = ctx_count // Y_HI
    y_hi = ctx_pos % Y_HI
    super_rows = Y_HI * tok_rows
    offsets = jnp.arange(tok_rows, dtype=jnp.int32)

    def terms(ahead_kv, behind_kv, turn, with_diagonal=False):
        ahead_owner = (z_pos + turn) % z_count
        behind_owner = (z_pos - turn) % z_count
        key_starts = (ahead_owner * super_rows, behind_owner * super_rows + tok_rows)
        key_pos = jnp.concatenate([key_starts[0] + offsets, key_starts[1] + offsets])
        live_mask = lax.optimization_barrier(
            live_region(block_mask, query_start, tok_rows, key_pos, key_starts, with_diagonal)
        )
        key_values = jnp.concatenate([ahead_kv, behind_kv], axis=0)
        query_term, key_term, value_term = contract(
            queries,
            out_grads,
            row_delta,
            log_sums,
            key_values[:, :HEAD_SIZE],
            key_values[:, HEAD_SIZE:],
            live_mask,
        )
        kv_term = jnp.concatenate([key_term, value_term], axis=1)
        return query_term, kv_term[:tok_rows], kv_term[tok_rows:]

    key_values = jnp.concatenate([key_matrix, value_matrix], axis=1)
    partner_kv = from_partner(key_values, ctx_count)
    ahead_kv = jnp.where(y_hi == 0, key_values, partner_kv)
    behind_kv = jnp.where(y_hi == 0, partner_kv, key_values)
    next_ahead = along_z(ahead_kv, ctx_count, 1)
    next_behind = along_z(behind_kv, ctx_count, -1)
    query_acc, ahead_pending, behind_pending = terms(ahead_kv, behind_kv, 0, with_diagonal=True)

    def visit_turn(turn, carried):
        ahead_kv, behind_kv, query_acc, ahead_pending, behind_pending = carried
        ahead_received = along_z(ahead_pending, ctx_count, 1)
        behind_received = along_z(behind_pending, ctx_count, -1)
        next_ahead = along_z(ahead_kv, ctx_count, 1)
        next_behind = along_z(behind_kv, ctx_count, -1)
        query_term, ahead_term, behind_term = terms(ahead_kv, behind_kv, turn)
        return (
            next_ahead,
            next_behind,
            query_acc + query_term,
            ahead_received + ahead_term,
            behind_received + behind_term,
        )

    ahead_kv, behind_kv, query_acc, ahead_pending, behind_pending = lax.fori_loop(
        1,
        z_count - 1,
        visit_turn,
        (next_ahead, next_behind, query_acc, ahead_pending, behind_pending),
    )
    ahead_received = along_z(ahead_pending, ctx_count, 1)
    behind_received = along_z(behind_pending, ctx_count, -1)
    query_term, ahead_term, behind_term = terms(ahead_kv, behind_kv, z_count - 1)
    query_acc = query_acc + query_term
    ahead_final = ahead_received + ahead_term
    behind_final = behind_received + behind_term
    same_ring = jnp.where(y_hi == 0, ahead_final, behind_final)
    other_ring = jnp.where(y_hi == 0, behind_final, ahead_final)
    summed = to_owner(same_ring, ctx_count, 0) + to_owner(other_ring, ctx_count, 1)
    logit_scale = 1.0 / math.sqrt(HEAD_SIZE)
    query_grad = (query_acc * logit_scale).reshape(tok_rows, col_width).astype(jnp.bfloat16)
    key_gradient = (summed[:, :HEAD_SIZE] * logit_scale).astype(jnp.bfloat16)
    value_gradient = summed[:, HEAD_SIZE:].astype(jnp.bfloat16)
    return (query_grad, key_gradient, value_gradient)


def solution(mesh):
    placed = (
        P(("dp", "ctx"), "tp"),
        P(("dp", "ctx"), "tp"),
        P(("dp", "ctx"), "tp"),
        P(("dp", "ctx"), "tp"),
        P(("dp", "ctx", "tp"), None),
        P("tp", ("dp", "ctx")),
        P("dp", None),
    )
    return jax.shard_map(
        local,
        mesh=mesh,
        in_specs=placed,
        out_specs=(P(("dp", "ctx"), "tp"), P(("dp", "ctx"), "tp"), P(("dp", "ctx"), "tp")),
        check_vma=False,
    )
```

```python
import math

import jax
import jax.numpy as jnp
from jax import lax
from jax.sharding import PartitionSpec as P

BLK = 128
HEAD_SIZE = 128
Y_HI = 2


def along_z(value, ctx_count, shift):
    z_count = ctx_count // Y_HI
    pairs = [
        (Y_HI * ((z + shift) % z_count) + h, Y_HI * z + h)
        for z in range(z_count)
        for h in range(Y_HI)
    ]
    return lax.ppermute(value, "ctx", pairs)


def to_owner(value, ctx_count, ring_half):
    z_count = ctx_count // Y_HI
    pairs = []
    for z in range(z_count):
        for h in range(Y_HI):
            first = (h == 0) == (ring_half == 0)
            target = Y_HI * ((z - 1) % z_count) if first else Y_HI * ((z + 1) % z_count) + 1
            pairs.append((Y_HI * z + h, target))
    return lax.ppermute(value, "ctx", pairs)


def from_partner(value, ctx_count):
    pairs = [(c, c ^ 1) for c in range(ctx_count)]
    return lax.ppermute(value, "ctx", pairs)


def live_region(block_mask, query_start, tok_rows, key_pos, key_starts, with_diagonal):
    row_count = tok_rows // BLK
    block_table = jnp.concatenate(
        [
            lax.dynamic_slice(block_mask, (query_start // BLK, start // BLK), (row_count, row_count))
            for start in key_starts
        ],
        axis=1,
    )
    if not with_diagonal:
        query_blocks = query_start // BLK + jnp.arange(row_count, dtype=jnp.int32)
        key_blocks = key_pos[::BLK] // BLK
        block_live = (key_blocks[None, :] < query_blocks[:, None]) & (block_table == 1)
        block_live = lax.optimization_barrier(block_live)
        return jnp.repeat(jnp.repeat(block_live, BLK, axis=0), BLK, axis=1)
    block_table = jnp.repeat(jnp.repeat(block_table, BLK, axis=0), BLK, axis=1)
    query_pos = query_start + jnp.arange(tok_rows, dtype=jnp.int32)
    query_block = (query_pos // BLK)[:, None]
    key_block = (key_pos // BLK)[None, :]
    earlier = (key_block < query_block) & (block_table == 1)
    diagonal = (key_block == query_block) & (key_pos[None, :] <= query_pos[:, None])
    return earlier | diagonal


def contract(queries, out_grads, row_delta, log_sums, keys_part, values_part, live_mask):
    logit_scale = 1.0 / math.sqrt(HEAD_SIZE)
    scores = (
        jnp.einsum("igd,jd->gij", queries, keys_part, preferred_element_type=jnp.float32)
        * logit_scale
    )
    probabilities = jnp.where(live_mask[None], jnp.exp(scores - log_sums[:, :, None]), 0.0)
    prob_grad = jnp.einsum(
        "igd,jd->gij", out_grads, values_part, preferred_element_type=jnp.float32
    )
    dscore = (probabilities * (prob_grad - row_delta[:, :, None])).astype(jnp.bfloat16)
    query_term = jnp.einsum("gij,jd->igd", dscore, keys_part, preferred_element_type=jnp.float32)
    key_term = jnp.einsum("gij,igd->jd", dscore, queries, preferred_element_type=jnp.float32)
    value_term = jnp.einsum(
        "gij,igd->jd",
        probabilities.astype(jnp.bfloat16),
        out_grads,
        preferred_element_type=jnp.float32,
    )
    return (query_term, key_term, value_term)


def local(query_rows, key_matrix, value_matrix, attn_out, out_grad, log_sums, block_mask):
    tok_rows = query_rows.shape[0]
    col_width = query_rows.shape[1]
    heads_local = col_width // HEAD_SIZE
    ctx_pos = lax.axis_index("ctx")
    ctx_count = lax.axis_size("ctx")
    tp_count = lax.axis_size("tp")
    grad_rows = out_grad.shape[0]
    pieces = out_grad.reshape(grad_rows, tp_count, col_width)
    own_grad = lax.all_to_all(pieces, "tp", split_axis=1, concat_axis=0, tiled=True)
    queries = query_rows.reshape(tok_rows, heads_local, HEAD_SIZE)
    out_grads = own_grad.reshape(tok_rows, heads_local, HEAD_SIZE)
    outputs = attn_out.reshape(tok_rows, heads_local, HEAD_SIZE)
    row_delta = jnp.sum(out_grads.astype(jnp.float32) * outputs.astype(jnp.float32), axis=2).T
    query_start = ctx_pos * tok_rows
    z_pos = ctx_pos // Y_HI
    z_count = ctx_count // Y_HI
    y_hi = ctx_pos % Y_HI
    super_rows = Y_HI * tok_rows
    offsets = jnp.arange(tok_rows, dtype=jnp.int32)

    def terms(ahead_kv, behind_kv, turn, with_diagonal=False):
        ahead_owner = (z_pos + turn) % z_count
        behind_owner = (z_pos - turn) % z_count
        key_starts = (ahead_owner * super_rows, behind_owner * super_rows + tok_rows)
        key_pos = jnp.concatenate([key_starts[0] + offsets, key_starts[1] + offsets])
        live_mask = live_region(block_mask, query_start, tok_rows, key_pos, key_starts, with_diagonal)
        if with_diagonal:
            live_mask = lax.optimization_barrier(live_mask)
        key_values = jnp.concatenate([ahead_kv, behind_kv], axis=0)
        query_term, key_term, value_term = contract(
            queries,
            out_grads,
            row_delta,
            log_sums,
            key_values[:, :HEAD_SIZE],
            key_values[:, HEAD_SIZE:],
            live_mask,
        )
        kv_term = jnp.concatenate([key_term, value_term], axis=1)
        return query_term, kv_term[:tok_rows], kv_term[tok_rows:]

    key_values = jnp.concatenate([key_matrix, value_matrix], axis=1)
    partner_kv = from_partner(key_values, ctx_count)
    ahead_kv = jnp.where(y_hi == 0, key_values, partner_kv)
    behind_kv = jnp.where(y_hi == 0, partner_kv, key_values)
    next_ahead = along_z(ahead_kv, ctx_count, 1)
    next_behind = along_z(behind_kv, ctx_count, -1)
    query_acc, ahead_pending, behind_pending = terms(ahead_kv, behind_kv, 0, with_diagonal=True)

    def visit_turn(turn, carried):
        ahead_kv, behind_kv, query_acc, ahead_pending, behind_pending = carried
        ahead_received = along_z(ahead_pending, ctx_count, 1)
        behind_received = along_z(behind_pending, ctx_count, -1)
        next_ahead = along_z(ahead_kv, ctx_count, 1)
        next_behind = along_z(behind_kv, ctx_count, -1)
        query_term, ahead_term, behind_term = terms(ahead_kv, behind_kv, turn)
        return (
            next_ahead,
            next_behind,
            query_acc + query_term,
            ahead_received + ahead_term,
            behind_received + behind_term,
        )

    ahead_kv, behind_kv, query_acc, ahead_pending, behind_pending = lax.fori_loop(
        1,
        z_count - 1,
        visit_turn,
        (next_ahead, next_behind, query_acc, ahead_pending, behind_pending),
    )
    ahead_received = along_z(ahead_pending, ctx_count, 1)
    behind_received = along_z(behind_pending, ctx_count, -1)
    query_term, ahead_term, behind_term = terms(ahead_kv, behind_kv, z_count - 1)
    query_acc = query_acc + query_term
    ahead_final = ahead_received + ahead_term
    behind_final = behind_received + behind_term
    same_ring = jnp.where(y_hi == 0, ahead_final, behind_final)
    other_ring = jnp.where(y_hi == 0, behind_final, ahead_final)
    summed = to_owner(same_ring, ctx_count, 0) + to_owner(other_ring, ctx_count, 1)
    logit_scale = 1.0 / math.sqrt(HEAD_SIZE)
    query_grad = (query_acc * logit_scale).reshape(tok_rows, col_width).astype(jnp.bfloat16)
    key_gradient = (summed[:, :HEAD_SIZE] * logit_scale).astype(jnp.bfloat16)
    value_gradient = summed[:, HEAD_SIZE:].astype(jnp.bfloat16)
    return (query_grad, key_gradient, value_gradient)


def solution(mesh):
    placed = (
        P(("dp", "ctx"), "tp"),
        P(("dp", "ctx"), "tp"),
        P(("dp", "ctx"), "tp"),
        P(("dp", "ctx"), "tp"),
        P(("dp", "ctx", "tp"), None),
        P("tp", ("dp", "ctx")),
        P("dp", None),
    )
    return jax.shard_map(
        local,
        mesh=mesh,
        in_specs=placed,
        out_specs=(P(("dp", "ctx"), "tp"), P(("dp", "ctx"), "tp"), P(("dp", "ctx"), "tp")),
        check_vma=False,
    )
```

```python
import math

import jax
import jax.numpy as jnp
from jax import lax
from jax.sharding import PartitionSpec as P

BLK = 128
HEAD_SIZE = 128
Y_HI = 2


def along_z(value, ctx_count, shift):
    z_count = ctx_count // Y_HI
    pairs = [
        (Y_HI * ((z + shift) % z_count) + h, Y_HI * z + h)
        for z in range(z_count)
        for h in range(Y_HI)
    ]
    return lax.ppermute(value, "ctx", pairs)


def to_owner(value, ctx_count, ring_half):
    z_count = ctx_count // Y_HI
    pairs = []
    for z in range(z_count):
        for h in range(Y_HI):
            first = (h == 0) == (ring_half == 0)
            target = Y_HI * ((z - 1) % z_count) if first else Y_HI * ((z + 1) % z_count) + 1
            pairs.append((Y_HI * z + h, target))
    return lax.ppermute(value, "ctx", pairs)


def from_partner(value, ctx_count):
    pairs = [(c, c ^ 1) for c in range(ctx_count)]
    return lax.ppermute(value, "ctx", pairs)


def live_region(block_mask, query_start, tok_rows, key_pos, key_starts, with_diagonal):
    row_count = tok_rows // BLK
    if not with_diagonal:
        block_table = None
    else:
        block_table = jnp.concatenate(
        [
            lax.dynamic_slice(block_mask, (query_start // BLK, start // BLK), (row_count, row_count))
            for start in key_starts
        ],
        axis=1,
    )
    if not with_diagonal:
        query_blocks = query_start // BLK + jnp.arange(row_count, dtype=jnp.int32)
        key_blocks = key_pos[::BLK] // BLK
        own_rows = lax.dynamic_slice_in_dim(block_mask, query_start // BLK, row_count, 0)
        picks = jnp.arange(block_mask.shape[1], dtype=jnp.int32)[None, :] == key_blocks[:, None]
        chosen = jnp.any((own_rows[:, None, :] == 1) & picks[None, :, :], axis=2)
        block_live = (key_blocks[None, :] < query_blocks[:, None]) & chosen
        block_live = lax.optimization_barrier(block_live)
        return jnp.repeat(jnp.repeat(block_live, BLK, axis=0), BLK, axis=1)
    block_table = jnp.repeat(jnp.repeat(block_table, BLK, axis=0), BLK, axis=1)
    query_pos = query_start + jnp.arange(tok_rows, dtype=jnp.int32)
    query_block = (query_pos // BLK)[:, None]
    key_block = (key_pos // BLK)[None, :]
    earlier = (key_block < query_block) & (block_table == 1)
    diagonal = (key_block == query_block) & (key_pos[None, :] <= query_pos[:, None])
    return earlier | diagonal


def contract(queries, out_grads, row_delta, log_sums, keys_part, values_part, live_mask):
    logit_scale = 1.0 / math.sqrt(HEAD_SIZE)
    scores = (
        jnp.einsum("igd,jd->gij", queries, keys_part, preferred_element_type=jnp.float32)
        * logit_scale
    )
    probabilities = jnp.where(live_mask[None], jnp.exp(scores - log_sums[:, :, None]), 0.0)
    prob_grad = jnp.einsum(
        "igd,jd->gij", out_grads, values_part, preferred_element_type=jnp.float32
    )
    dscore = (probabilities * (prob_grad - row_delta[:, :, None])).astype(jnp.bfloat16)
    query_term = jnp.einsum("gij,jd->igd", dscore, keys_part, preferred_element_type=jnp.float32)
    key_term = jnp.einsum("gij,igd->jd", dscore, queries, preferred_element_type=jnp.float32)
    value_term = jnp.einsum(
        "gij,igd->jd",
        probabilities.astype(jnp.bfloat16),
        out_grads,
        preferred_element_type=jnp.float32,
    )
    return (query_term, key_term, value_term)


def local(query_rows, key_matrix, value_matrix, attn_out, out_grad, log_sums, block_mask):
    tok_rows = query_rows.shape[0]
    col_width = query_rows.shape[1]
    heads_local = col_width // HEAD_SIZE
    ctx_pos = lax.axis_index("ctx")
    ctx_count = lax.axis_size("ctx")
    tp_count = lax.axis_size("tp")
    grad_rows = out_grad.shape[0]
    pieces = out_grad.reshape(grad_rows, tp_count, col_width)
    own_grad = lax.all_to_all(pieces, "tp", split_axis=1, concat_axis=0, tiled=True)
    queries = query_rows.reshape(tok_rows, heads_local, HEAD_SIZE)
    out_grads = own_grad.reshape(tok_rows, heads_local, HEAD_SIZE)
    outputs = attn_out.reshape(tok_rows, heads_local, HEAD_SIZE)
    row_delta = jnp.sum(out_grads.astype(jnp.float32) * outputs.astype(jnp.float32), axis=2).T
    query_start = ctx_pos * tok_rows
    z_pos = ctx_pos // Y_HI
    z_count = ctx_count // Y_HI
    y_hi = ctx_pos % Y_HI
    super_rows = Y_HI * tok_rows
    offsets = jnp.arange(tok_rows, dtype=jnp.int32)

    def terms(ahead_kv, behind_kv, turn, with_diagonal=False):
        ahead_owner = (z_pos + turn) % z_count
        behind_owner = (z_pos - turn) % z_count
        key_starts = (ahead_owner * super_rows, behind_owner * super_rows + tok_rows)
        key_pos = jnp.concatenate([key_starts[0] + offsets, key_starts[1] + offsets])
        live_mask = live_region(block_mask, query_start, tok_rows, key_pos, key_starts, with_diagonal)
        if with_diagonal:
            live_mask = lax.optimization_barrier(live_mask)
        key_values = jnp.concatenate([ahead_kv, behind_kv], axis=0)
        query_term, key_term, value_term = contract(
            queries,
            out_grads,
            row_delta,
            log_sums,
            key_values[:, :HEAD_SIZE],
            key_values[:, HEAD_SIZE:],
            live_mask,
        )
        kv_term = jnp.concatenate([key_term, value_term], axis=1)
        return query_term, kv_term[:tok_rows], kv_term[tok_rows:]

    key_values = jnp.concatenate([key_matrix, value_matrix], axis=1)
    partner_kv = from_partner(key_values, ctx_count)
    ahead_kv = jnp.where(y_hi == 0, key_values, partner_kv)
    behind_kv = jnp.where(y_hi == 0, partner_kv, key_values)
    next_ahead = along_z(ahead_kv, ctx_count, 1)
    next_behind = along_z(behind_kv, ctx_count, -1)
    query_acc, ahead_pending, behind_pending = terms(ahead_kv, behind_kv, 0, with_diagonal=True)

    def visit_turn(turn, carried):
        ahead_kv, behind_kv, query_acc, ahead_pending, behind_pending = carried
        ahead_received = along_z(ahead_pending, ctx_count, 1)
        behind_received = along_z(behind_pending, ctx_count, -1)
        next_ahead = along_z(ahead_kv, ctx_count, 1)
        next_behind = along_z(behind_kv, ctx_count, -1)
        query_term, ahead_term, behind_term = terms(ahead_kv, behind_kv, turn)
        return (
            next_ahead,
            next_behind,
            query_acc + query_term,
            ahead_received + ahead_term,
            behind_received + behind_term,
        )

    ahead_kv, behind_kv, query_acc, ahead_pending, behind_pending = lax.fori_loop(
        1,
        z_count - 1,
        visit_turn,
        (next_ahead, next_behind, query_acc, ahead_pending, behind_pending),
    )
    ahead_received = along_z(ahead_pending, ctx_count, 1)
    behind_received = along_z(behind_pending, ctx_count, -1)
    query_term, ahead_term, behind_term = terms(ahead_kv, behind_kv, z_count - 1)
    query_acc = query_acc + query_term
    ahead_final = ahead_received + ahead_term
    behind_final = behind_received + behind_term
    same_ring = jnp.where(y_hi == 0, ahead_final, behind_final)
    other_ring = jnp.where(y_hi == 0, behind_final, ahead_final)
    summed = to_owner(same_ring, ctx_count, 0) + to_owner(other_ring, ctx_count, 1)
    logit_scale = 1.0 / math.sqrt(HEAD_SIZE)
    query_grad = (query_acc * logit_scale).reshape(tok_rows, col_width).astype(jnp.bfloat16)
    key_gradient = (summed[:, :HEAD_SIZE] * logit_scale).astype(jnp.bfloat16)
    value_gradient = summed[:, HEAD_SIZE:].astype(jnp.bfloat16)
    return (query_grad, key_gradient, value_gradient)


def solution(mesh):
    placed = (
        P(("dp", "ctx"), "tp"),
        P(("dp", "ctx"), "tp"),
        P(("dp", "ctx"), "tp"),
        P(("dp", "ctx"), "tp"),
        P(("dp", "ctx", "tp"), None),
        P("tp", ("dp", "ctx")),
        P("dp", None),
    )
    return jax.shard_map(
        local,
        mesh=mesh,
        in_specs=placed,
        out_specs=(P(("dp", "ctx"), "tp"), P(("dp", "ctx"), "tp"), P(("dp", "ctx"), "tp")),
        check_vma=False,
    )
```

```python
import math

import jax
import jax.numpy as jnp
from jax import lax
from jax.sharding import PartitionSpec as P

BLK = 128
HEAD_SIZE = 128
Y_HI = 2


def along_z(value, ctx_count, shift):
    z_count = ctx_count // Y_HI
    pairs = [
        (Y_HI * ((z + shift) % z_count) + h, Y_HI * z + h)
        for z in range(z_count)
        for h in range(Y_HI)
    ]
    return lax.ppermute(value, "ctx", pairs)


def to_owner(value, ctx_count, ring_half):
    z_count = ctx_count // Y_HI
    pairs = []
    for z in range(z_count):
        for h in range(Y_HI):
            first = (h == 0) == (ring_half == 0)
            target = Y_HI * ((z - 1) % z_count) if first else Y_HI * ((z + 1) % z_count) + 1
            pairs.append((Y_HI * z + h, target))
    return lax.ppermute(value, "ctx", pairs)


def from_partner(value, ctx_count):
    pairs = [(c, c ^ 1) for c in range(ctx_count)]
    return lax.ppermute(value, "ctx", pairs)


def live_region(block_mask, query_start, tok_rows, key_pos, key_starts, with_diagonal):
    row_count = tok_rows // BLK
    block_table = jnp.concatenate(
        [
            lax.dynamic_slice(block_mask, (query_start // BLK, start // BLK), (row_count, row_count))
            for start in key_starts
        ],
        axis=1,
    )
    if not with_diagonal:
        query_blocks = query_start // BLK + jnp.arange(row_count, dtype=jnp.int32)
        key_blocks = key_pos[::BLK] // BLK
        block_live = (key_blocks[None, :] < query_blocks[:, None]) & (block_table == 1)
        return block_live
    block_table = jnp.repeat(jnp.repeat(block_table, BLK, axis=0), BLK, axis=1)
    query_pos = query_start + jnp.arange(tok_rows, dtype=jnp.int32)
    query_block = (query_pos // BLK)[:, None]
    key_block = (key_pos // BLK)[None, :]
    earlier = (key_block < query_block) & (block_table == 1)
    diagonal = (key_block == query_block) & (key_pos[None, :] <= query_pos[:, None])
    return earlier | diagonal


def contract(queries, out_grads, row_delta, log_sums, keys_part, values_part, live_mask):
    logit_scale = 1.0 / math.sqrt(HEAD_SIZE)
    scores = (
        jnp.einsum("igd,jd->gij", queries, keys_part, preferred_element_type=jnp.float32)
        * logit_scale
    )
    probabilities = jnp.where(live_mask[None], jnp.exp(scores - log_sums[:, :, None]), 0.0)
    prob_grad = jnp.einsum(
        "igd,jd->gij", out_grads, values_part, preferred_element_type=jnp.float32
    )
    dscore = (probabilities * (prob_grad - row_delta[:, :, None])).astype(jnp.bfloat16)
    query_term = jnp.einsum("gij,jd->igd", dscore, keys_part, preferred_element_type=jnp.float32)
    key_term = jnp.einsum("gij,igd->jd", dscore, queries, preferred_element_type=jnp.float32)
    value_term = jnp.einsum(
        "gij,igd->jd",
        probabilities.astype(jnp.bfloat16),
        out_grads,
        preferred_element_type=jnp.float32,
    )
    return (query_term, key_term, value_term)


def local(query_rows, key_matrix, value_matrix, attn_out, out_grad, log_sums, block_mask):
    tok_rows = query_rows.shape[0]
    col_width = query_rows.shape[1]
    heads_local = col_width // HEAD_SIZE
    ctx_pos = lax.axis_index("ctx")
    ctx_count = lax.axis_size("ctx")
    tp_count = lax.axis_size("tp")
    grad_rows = out_grad.shape[0]
    pieces = out_grad.reshape(grad_rows, tp_count, col_width)
    own_grad = lax.all_to_all(pieces, "tp", split_axis=1, concat_axis=0, tiled=True)
    queries = query_rows.reshape(tok_rows, heads_local, HEAD_SIZE)
    out_grads = own_grad.reshape(tok_rows, heads_local, HEAD_SIZE)
    outputs = attn_out.reshape(tok_rows, heads_local, HEAD_SIZE)
    row_delta = jnp.sum(out_grads.astype(jnp.float32) * outputs.astype(jnp.float32), axis=2).T
    query_start = ctx_pos * tok_rows
    z_pos = ctx_pos // Y_HI
    z_count = ctx_count // Y_HI
    y_hi = ctx_pos % Y_HI
    super_rows = Y_HI * tok_rows
    offsets = jnp.arange(tok_rows, dtype=jnp.int32)

    def turn_table(turn):
        ahead_owner = (z_pos + turn) % z_count
        behind_owner = (z_pos - turn) % z_count
        key_starts = (ahead_owner * super_rows, behind_owner * super_rows + tok_rows)
        key_pos = jnp.concatenate([key_starts[0] + offsets, key_starts[1] + offsets])
        return live_region(block_mask, query_start, tok_rows, key_pos, key_starts, False)

    turn_ids = jnp.arange(z_count, dtype=jnp.int32)
    all_tables = jax.vmap(turn_table)(turn_ids)

    def terms(ahead_kv, behind_kv, turn, with_diagonal=False):
        ahead_owner = (z_pos + turn) % z_count
        behind_owner = (z_pos - turn) % z_count
        key_starts = (ahead_owner * super_rows, behind_owner * super_rows + tok_rows)
        key_pos = jnp.concatenate([key_starts[0] + offsets, key_starts[1] + offsets])
        if with_diagonal:
            live_mask = lax.optimization_barrier(
                live_region(block_mask, query_start, tok_rows, key_pos, key_starts, True)
            )
        else:
            chosen = (turn_ids == turn)[:, None, None] & all_tables
            block_live = lax.optimization_barrier(jnp.any(chosen, axis=0))
            live_mask = jnp.repeat(jnp.repeat(block_live, BLK, axis=0), BLK, axis=1)
        key_values = jnp.concatenate([ahead_kv, behind_kv], axis=0)
        query_term, key_term, value_term = contract(
            queries,
            out_grads,
            row_delta,
            log_sums,
            key_values[:, :HEAD_SIZE],
            key_values[:, HEAD_SIZE:],
            live_mask,
        )
        kv_term = jnp.concatenate([key_term, value_term], axis=1)
        return query_term, kv_term[:tok_rows], kv_term[tok_rows:]

    key_values = jnp.concatenate([key_matrix, value_matrix], axis=1)
    partner_kv = from_partner(key_values, ctx_count)
    ahead_kv = jnp.where(y_hi == 0, key_values, partner_kv)
    behind_kv = jnp.where(y_hi == 0, partner_kv, key_values)
    next_ahead = along_z(ahead_kv, ctx_count, 1)
    next_behind = along_z(behind_kv, ctx_count, -1)
    query_acc, ahead_pending, behind_pending = terms(ahead_kv, behind_kv, 0, with_diagonal=True)

    def visit_turn(turn, carried):
        ahead_kv, behind_kv, query_acc, ahead_pending, behind_pending = carried
        ahead_received = along_z(ahead_pending, ctx_count, 1)
        behind_received = along_z(behind_pending, ctx_count, -1)
        next_ahead = along_z(ahead_kv, ctx_count, 1)
        next_behind = along_z(behind_kv, ctx_count, -1)
        query_term, ahead_term, behind_term = terms(ahead_kv, behind_kv, turn)
        return (
            next_ahead,
            next_behind,
            query_acc + query_term,
            ahead_received + ahead_term,
            behind_received + behind_term,
        )

    ahead_kv, behind_kv, query_acc, ahead_pending, behind_pending = lax.fori_loop(
        1,
        z_count - 1,
        visit_turn,
        (next_ahead, next_behind, query_acc, ahead_pending, behind_pending),
    )
    ahead_received = along_z(ahead_pending, ctx_count, 1)
    behind_received = along_z(behind_pending, ctx_count, -1)
    query_term, ahead_term, behind_term = terms(ahead_kv, behind_kv, z_count - 1)
    query_acc = query_acc + query_term
    ahead_final = ahead_received + ahead_term
    behind_final = behind_received + behind_term
    same_ring = jnp.where(y_hi == 0, ahead_final, behind_final)
    other_ring = jnp.where(y_hi == 0, behind_final, ahead_final)
    summed = to_owner(same_ring, ctx_count, 0) + to_owner(other_ring, ctx_count, 1)
    logit_scale = 1.0 / math.sqrt(HEAD_SIZE)
    query_grad = (query_acc * logit_scale).reshape(tok_rows, col_width).astype(jnp.bfloat16)
    key_gradient = (summed[:, :HEAD_SIZE] * logit_scale).astype(jnp.bfloat16)
    value_gradient = summed[:, HEAD_SIZE:].astype(jnp.bfloat16)
    return (query_grad, key_gradient, value_gradient)


def solution(mesh):
    placed = (
        P(("dp", "ctx"), "tp"),
        P(("dp", "ctx"), "tp"),
        P(("dp", "ctx"), "tp"),
        P(("dp", "ctx"), "tp"),
        P(("dp", "ctx", "tp"), None),
        P("tp", ("dp", "ctx")),
        P("dp", None),
    )
    return jax.shard_map(
        local,
        mesh=mesh,
        in_specs=placed,
        out_specs=(P(("dp", "ctx"), "tp"), P(("dp", "ctx"), "tp"), P(("dp", "ctx"), "tp")),
        check_vma=False,
    )
```
